128 devices in a mesh: tm: 32 (over x, z, core), chan: 4 (over y).
Axes of the slice: x: 4, y: 4, z: 4, core: 2. Of those that a mesh axis runs over, the one named last changes fastest.
Arguments:
- inputs: bfloat16 [64, 256, 512], P('tm'), may hold values from -6 to 6
- decay: float32 [64, 512], P('tm', 'chan'), may hold values from 0 to 1, as said below
- kernel_b: bfloat16 [9, 512, 256], P(None, 'chan'), may hold values from -0.125 to 0.125
- kernel_c: bfloat16 [9, 256, 512], P(None, 'chan'), may hold values from -0.09375 to 0.09375
- cotangent: bfloat16 [64, 256, 512], P('tm', 'chan'), may hold values from -0.03125 to 0.03125
Outputs:
- grad_b: float32 [9, 512, 256], P(None, 'chan')
- grad_c: float32 [9, 256, 512], P(None, 'chan')
- decay_grad: float32 [64, 512], P('tm', 'chan')
The draws below stay inside these ranges and needn't reach their ends.
Inputs may be any that keep to these rules, and one draw needn't show every extreme that they name: decay lies strictly between 0 and 1.
All inputs are finite; a program needn't handle non-finite values.
Results may differ from the reference program's by a relative error of at most 0.003.
Values may be sent and summed in bfloat16 or wider, within the bound.
No kernel may reach another device: no remote copies, remote signals or barrier semaphores. Data moves between devices by JAX's collectives and lax.ppermute only.
A program may use at most 128 MiB of HBM per device.

```python
import jax
import jax.numpy as jnp
from jax import lax

U = 256
STATE_CHANNELS = 512
W = 64
H = 8
TOTAL_FRAMES = 64


def draw_decay(key, part):
    random_keys = jax.random.split(key, 6)
    slow_share = 5
    slow = jax.random.randint(random_keys[0], (STATE_CHANNELS,), 0, 10) < slow_share
    rate_slow = jax.random.uniform(random_keys[1], (STATE_CHANNELS,), jnp.float32, 0.3, 1.5) / TOTAL_FRAMES
    rate_fast = jax.random.uniform(random_keys[2], (STATE_CHANNELS,), jnp.float32, 0.15, 0.5)
    rates = jnp.where(slow, rate_slow, rate_fast)
    jitter = jnp.exp(jax.random.uniform(random_keys[3], (TOTAL_FRAMES, STATE_CHANNELS), jnp.float32, -0.35, 0.35))
    frame_groups = jax.random.randint(random_keys[4], (3,), 0, TOTAL_FRAMES)
    marked_rows = jnp.any(jnp.arange(TOTAL_FRAMES)[:, None] == frame_groups[None, :], axis=1)
    depth = jax.random.uniform(random_keys[5], (TOTAL_FRAMES, 1), jnp.float32, 0.5, 0.8)
    decay_factor = jnp.where(marked_rows[:, None], depth, 1.0)
    return (jnp.exp(-rates[None, :] * jitter) * decay_factor).astype(jnp.float32)


def shard_levels(rng, dims, shards, least, top_value):
    gain, own = 1.0, jax.random.fold_in(rng, 6)
    for position, shards_of in shards:
        draws = jnp.exp(jax.random.uniform(jax.random.fold_in(own, position), (shards_of,), jnp.float32, least / len(shards), top_value / len(shards)))
        gain = gain * jnp.repeat(draws, dims[position] // shards_of).reshape([-1 if axis == position else 1 for axis in range(len(dims))])
    return gain


def centred(key, extent, scale, reach, shards=(), kind=jnp.bfloat16):
    result = jax.random.normal(key, extent, jnp.float32) * scale
    if len(shards) > 0:
        result = shard_levels(key, extent, shards, -0.22, 0.18) * result
    return jnp.clip(result, min=-reach, max=reach).astype(kind)


def setup_inputs(seed: int = 0) -> dict:
    splits = jax.random.split(jax.random.key(seed), 6)
    inputs = centred(splits[0], (TOTAL_FRAMES, U, H * W), 1.0, 6.0, ((0, 32),))
    decay = draw_decay(jax.random.fold_in(splits[5], 71), 0)
    kernel_b = centred(splits[2], (9, STATE_CHANNELS, U), (9 * U) ** -0.5, 0.125, ((1, 4),))
    kernel_c = centred(splits[3], (9, U, STATE_CHANNELS), (9 * STATE_CHANNELS) ** -0.5, 0.09375, ((1, 4),))
    cotangent = centred(splits[4], (TOTAL_FRAMES, U, H * W), ((TOTAL_FRAMES * H * W) ** -0.5), 0.03125, ((0, 32), (1, 4)))
    return {"inputs": inputs, "decay": decay, "kernel_b": kernel_b, "kernel_c": kernel_c, "cotangent": cotangent}


offsets = ((-1, -1), (-1, 0), (-1, 1), (0, -1), (0, 0), (0, 1), (1, -1), (1, 0), (1, 1))


def shift_cells(source, row_shift, col_shift, grid_width):
    cell_count = source.shape[-1]
    margin = grid_width + 1
    padded = jnp.pad(source, [(0, 0)] * (source.ndim - 1) + [(margin, margin)])
    first_cell = margin + row_shift * grid_width + col_shift
    shifted = lax.slice_in_dim(padded, first_cell, first_cell + cell_count, axis=source.ndim - 1)
    column = jnp.arange(cell_count) % grid_width
    inside = (column + col_shift >= 0) & (column + col_shift < grid_width)
    return jnp.where(inside, shifted, jnp.zeros((), source.dtype))


def stencil_stack(source, grid_width, decay_factor):
    parts = [shift_cells(source, decay_factor * pair[0], decay_factor * pair[1], grid_width) for pair in offsets]
    return jnp.stack(parts, axis=source.ndim - 2)


def reference(inputs, decay, kernel_b, kernel_c, cotangent):
    weight_b = kernel_b.astype(jnp.float32)
    weight_c = kernel_c.astype(jnp.float32)
    cell_count = inputs.shape[-1]

    def advance(current, frame_pair):
        input_frame, frame_rate = frame_pair
        input_stack = stencil_stack(input_frame, W, 1).astype(jnp.float32)
        drive = jnp.einsum('kpc,kcs->ps', weight_b, input_stack)
        current = frame_rate[:, None] * current + drive
        return current, current

    final_state, states = lax.scan(advance, jnp.zeros((STATE_CHANNELS, cell_count), jnp.float32), (inputs, decay))
    previous = jnp.concatenate([jnp.zeros((1, STATE_CHANNELS, cell_count), jnp.float32), states[:-1]], axis=0)

    def retreat(carry_all, frame_pair):
        carried, grad_b, grad_c = carry_all
        input_frame, frame_rate, frame_cot, frame_state, frame_prev = frame_pair
        cot_stack = stencil_stack(frame_cot, W, -1).astype(jnp.float32)
        injected = jnp.einsum('kup,kus->ps', weight_c, cot_stack)
        adjoint = injected + carried
        adjoint_bf = lax.optimization_barrier(adjoint.astype(jnp.bfloat16)).astype(jnp.float32)
        input_stack = stencil_stack(input_frame, W, 1).astype(jnp.float32)
        grad_b = grad_b + jnp.einsum('ps,kcs->kpc', adjoint_bf, input_stack)
        state_bf = lax.optimization_barrier(frame_state.astype(jnp.bfloat16)).astype(jnp.float32)
        state_stack = stencil_stack(state_bf, W, 1)
        grad_c = grad_c + jnp.einsum('us,kps->kup', frame_cot.astype(jnp.float32), state_stack)
        decay_row = jnp.sum(adjoint * frame_prev, axis=1)
        return (frame_rate[:, None] * adjoint, grad_b, grad_c), decay_row

    start = (jnp.zeros((STATE_CHANNELS, cell_count), jnp.float32), jnp.zeros((9, STATE_CHANNELS, U), jnp.float32), jnp.zeros((9, U, STATE_CHANNELS), jnp.float32))
    ending, decay_grad = lax.scan(retreat, start, (inputs, decay, cotangent, states, previous), reverse=True)
    return ending[1], ending[2], decay_grad
```

```python
import jax
import jax.numpy as jnp
from jax import lax
from jax.sharding import PartitionSpec as P

W = 64


offsets = ((-1, -1), (-1, 0), (-1, 1), (0, -1), (0, 0), (0, 1), (1, -1), (1, 0), (1, 1))


def passed_along(value, axis, steps):
    count = lax.axis_size(axis)
    first, last = (max(0, -steps), min(count, count - steps))
    return lax.ppermute(value, axis, [(source, source + steps) for source in range(first, last)])


def exclusive_scan(factor, value, axis, direction):
    rows = value.shape[0]
    packed = jnp.concatenate([value, jnp.pad(factor, (0, value.shape[1] - rows))[None]], axis=0)
    packed = passed_along(packed, axis, direction)
    distance = 1
    while distance < lax.axis_size(axis):
        arrived = passed_along(packed, axis, direction * distance)
        scale = packed[rows, :rows]
        combined_value = scale[:, None] * arrived[:rows] + packed[:rows]
        combined_factor = packed[rows] * arrived[rows]
        packed = jnp.concatenate([combined_value, combined_factor[None]], axis=0)
        distance *= 2
    return packed[:rows]


def shift_cells(source, row_shift, col_shift, grid_width):
    cell_count = source.shape[-1]
    margin = grid_width + 1
    padded = jnp.pad(source, [(0, 0)] * (source.ndim - 1) + [(margin, margin)])
    first_cell = margin + row_shift * grid_width + col_shift
    shifted = lax.slice_in_dim(padded, first_cell, first_cell + cell_count, axis=source.ndim - 1)
    column = jnp.arange(cell_count) % grid_width
    inside = (column + col_shift >= 0) & (column + col_shift < grid_width)
    return jnp.where(inside, shifted, jnp.zeros((), source.dtype))


def stencil_stack(source, grid_width, decay_factor):
    parts = [
        shift_cells(source, decay_factor * pair[0], decay_factor * pair[1], grid_width)
        for pair in offsets
    ]
    return jnp.stack(parts, axis=source.ndim - 2)


def body(inputs, decay, kernel_b, kernel_c, cotangent):
    local_rows = kernel_b.shape[1]
    cell_count = inputs.shape[-1]
    blank_state = jnp.zeros((local_rows, cell_count), jnp.float32)
    input_stack = stencil_stack(inputs, W, 1)
    drives = jnp.einsum("kpc,fkcs->fps", kernel_b, input_stack, preferred_element_type=jnp.float32)

    def advance(current, frame_pair):
        frame_rate, drive = frame_pair
        current = frame_rate[:, None] * current + drive
        return (current, current)

    local_end, local_states = lax.scan(advance, blank_state, (decay, drives))
    decay_total = jnp.prod(decay, axis=0)
    entering = exclusive_scan(decay_total, local_end, "tm", 1)
    cumulative = jnp.cumprod(decay, axis=0)
    states = local_states + cumulative[:, :, None] * entering[None]
    previous = jnp.concatenate([entering[None], states[:-1]], axis=0)
    states_bf = states.astype(jnp.bfloat16)
    cot_stack = stencil_stack(cotangent, W, -1)
    injected = lax.psum_scatter(
        jnp.einsum("kup,fkus->pfs", kernel_c, cot_stack, preferred_element_type=jnp.float32),
        "chan",
        scatter_dimension=0,
        tiled=True,
    )
    injected = jnp.moveaxis(injected, 1, 0)

    def retreat(carried, frame_pair):
        frame_rate, source = frame_pair
        adjoint = source + carried
        return (frame_rate[:, None] * adjoint, adjoint)

    message, local_adjoint = lax.scan(retreat, blank_state, (decay, injected), reverse=True)

    arriving = exclusive_scan(decay_total, message, "tm", -1)
    suffix = jnp.flip(jnp.cumprod(jnp.flip(decay, 0), 0), 0)
    later_decay = jnp.concatenate([suffix[1:], jnp.ones_like(decay[:1])], axis=0)
    adjoint = local_adjoint + later_decay[:, :, None] * arriving[None]
    decay_grad = jnp.sum(adjoint * previous, axis=2)
    adjoint_bf = adjoint.astype(jnp.bfloat16)
    grad_b_part = jnp.einsum(
        "fps,fkcs->kpc", adjoint_bf, input_stack, preferred_element_type=jnp.float32
    )
    shifted = stencil_stack(lax.all_gather(states_bf, "chan", axis=1, tiled=True), W, 1)
    grad_c_part = jnp.einsum(
        "fus,fkps->kup", cotangent, shifted, preferred_element_type=jnp.float32
    )
    grad_b, grad_c = lax.psum((grad_b_part, grad_c_part), "tm")
    return (grad_b, grad_c, decay_grad)


def solution(mesh):
    in_specs = (
        P("tm", None, None),
        P("tm", "chan"),
        P(None, "chan", None),
        P(None, "chan", None),
        P("tm", "chan", None),
    )
    out_specs = (P(None, "chan", None), P(None, "chan", None), P("tm", "chan"))
    return jax.shard_map(body, mesh=mesh, in_specs=in_specs, out_specs=out_specs, check_vma=False)
```

```python
import jax
import jax.numpy as jnp
from jax import lax
from jax.sharding import PartitionSpec as P

W = 64


offsets = ((-1, -1), (-1, 0), (-1, 1), (0, -1), (0, 0), (0, 1), (1, -1), (1, 0), (1, 1))


def passed_along(value, axis, steps):
    count = lax.axis_size(axis)
    first, last = (max(0, -steps), min(count, count - steps))
    return lax.ppermute(value, axis, [(source, source + steps) for source in range(first, last)])


def scan_chunks(factor, value, reverse):
    count = value.shape[0]
    distance = 1
    while distance < count:
        if reverse:
            pads = ((0, distance), (0, 0), (0, 0))
            earlier_value = jnp.pad(value[distance:], pads)
            earlier_factor = jnp.pad(factor[distance:], pads)
        else:
            pads = ((distance, 0), (0, 0), (0, 0))
            earlier_value = jnp.pad(value[:-distance], pads)
            earlier_factor = jnp.pad(factor[:-distance], pads)
        value = value + factor * earlier_value
        factor = factor * earlier_factor
        distance *= 2
    return value


def block_scans(factor, forward_value, backward_value, axis):
    count = lax.axis_size(axis)
    rows, cells = forward_value.shape
    chunk = rows // count
    factor_row = jnp.pad(factor.reshape(count, chunk), ((0, 0), (0, cells - chunk)))[:, None, :]
    packed = jnp.concatenate(
        [forward_value.reshape(count, chunk, cells), backward_value.reshape(count, chunk, cells), factor_row], axis=1
    )
    gathered = lax.all_to_all(packed, axis, 0, 0, tiled=True)
    block_factor = gathered[:, 2 * chunk, :chunk][:, :, None]
    forward_total = scan_chunks(block_factor, gathered[:, :chunk], False)
    backward_total = scan_chunks(block_factor, gathered[:, chunk : 2 * chunk], True)
    entering = jnp.pad(forward_total[:-1], ((1, 0), (0, 0), (0, 0)))
    arriving = jnp.pad(backward_total[1:], ((0, 1), (0, 0), (0, 0)))
    returned = lax.all_to_all(jnp.concatenate([entering, arriving], axis=1), axis, 0, 0, tiled=True)
    return returned[:, :chunk].reshape(rows, cells), returned[:, chunk:].reshape(rows, cells)


def shift_cells(source, row_shift, col_shift, grid_width):
    cell_count = source.shape[-1]
    margin = grid_width + 1
    padded = jnp.pad(source, [(0, 0)] * (source.ndim - 1) + [(margin, margin)])
    first_cell = margin + row_shift * grid_width + col_shift
    shifted = lax.slice_in_dim(padded, first_cell, first_cell + cell_count, axis=source.ndim - 1)
    column = jnp.arange(cell_count) % grid_width
    inside = (column + col_shift >= 0) & (column + col_shift < grid_width)
    return jnp.where(inside, shifted, jnp.zeros((), source.dtype))


def stencil_stack(source, grid_width, decay_factor):
    parts = [
        shift_cells(source, decay_factor * pair[0], decay_factor * pair[1], grid_width)
        for pair in offsets
    ]
    return jnp.stack(parts, axis=source.ndim - 2)


def body(inputs, decay, kernel_b, kernel_c, cotangent):
    local_rows = kernel_b.shape[1]
    cell_count = inputs.shape[-1]
    blank_state = jnp.zeros((local_rows, cell_count), jnp.float32)
    input_stack = stencil_stack(inputs, W, 1)
    drives = jnp.einsum("kpc,fkcs->fps", kernel_b, input_stack, preferred_element_type=jnp.float32)

    def advance(current, frame_pair):
        frame_rate, drive = frame_pair
        current = frame_rate[:, None] * current + drive
        return (current, current)

    local_end, local_states = lax.scan(advance, blank_state, (decay, drives))
    decay_total = jnp.prod(decay, axis=0)
    cot_stack = stencil_stack(cotangent, W, -1)
    injected = lax.psum_scatter(
        jnp.einsum("kup,fkus->pfs", kernel_c, cot_stack, preferred_element_type=jnp.float32),
        "chan",
        scatter_dimension=0,
        tiled=True,
    )
    injected = jnp.moveaxis(injected, 1, 0)

    def retreat(carried, frame_pair):
        frame_rate, source = frame_pair
        adjoint = source + carried
        return (frame_rate[:, None] * adjoint, adjoint)

    message, local_adjoint = lax.scan(retreat, blank_state, (decay, injected), reverse=True)

    entering, arriving = block_scans(decay_total, local_end, message, "tm")
    cumulative = jnp.cumprod(decay, axis=0)
    states = local_states + cumulative[:, :, None] * entering[None]
    previous = jnp.concatenate([entering[None], states[:-1]], axis=0)
    states_bf = states.astype(jnp.bfloat16)
    suffix = jnp.flip(jnp.cumprod(jnp.flip(decay, 0), 0), 0)
    later_decay = jnp.concatenate([suffix[1:], jnp.ones_like(decay[:1])], axis=0)
    adjoint = local_adjoint + later_decay[:, :, None] * arriving[None]
    decay_grad = jnp.sum(adjoint * previous, axis=2)
    adjoint_bf = adjoint.astype(jnp.bfloat16)
    grad_b_part = jnp.einsum(
        "fps,fkcs->kpc", adjoint_bf, input_stack, preferred_element_type=jnp.float32
    )
    shifted = stencil_stack(lax.all_gather(states_bf, "chan", axis=1, tiled=True), W, 1)
    grad_c_part = jnp.einsum(
        "fus,fkps->kup", cotangent, shifted, preferred_element_type=jnp.float32
    )
    grad_b, grad_c = lax.psum((grad_b_part, grad_c_part), "tm")
    return (grad_b, grad_c, decay_grad)


def solution(mesh):
    in_specs = (
        P("tm", None, None),
        P("tm", "chan"),
        P(None, "chan", None),
        P(None, "chan", None),
        P("tm", "chan", None),
    )
    out_specs = (P(None, "chan", None), P(None, "chan", None), P("tm", "chan"))
    return jax.shard_map(body, mesh=mesh, in_specs=in_specs, out_specs=out_specs, check_vma=False)
```

```python
import jax
import jax.numpy as jnp
from jax import lax
from jax.sharding import Mesh, PartitionSpec as P

W = 64


offsets = ((-1, -1), (-1, 0), (-1, 1), (0, -1), (0, 0), (0, 1), (1, -1), (1, 0), (1, 1))


def passed_along(value, axis, steps):
    count = lax.axis_size(axis)
    first, last = (max(0, -steps), min(count, count - steps))
    return lax.ppermute(value, axis, [(source, source + steps) for source in range(first, last)])


def scan_chunks(factor, value, reverse):
    count = value.shape[0]
    distance = 1
    while distance < count:
        if reverse:
            pads = ((0, distance), (0, 0), (0, 0))
            earlier_value = jnp.pad(value[distance:], pads)
            earlier_factor = jnp.pad(factor[distance:], pads)
        else:
            pads = ((distance, 0), (0, 0), (0, 0))
            earlier_value = jnp.pad(value[:-distance], pads)
            earlier_factor = jnp.pad(factor[:-distance], pads)
        value = value + factor * earlier_value
        factor = factor * earlier_factor
        distance *= 2
    return value


def block_scans(factor, forward_value, backward_value, axis):
    count = lax.axis_size(axis)
    rows, cells = forward_value.shape
    chunk = rows // count
    factor_row = jnp.pad(factor.reshape(count, chunk), ((0, 0), (0, cells - chunk)))[:, None, :]
    packed = jnp.concatenate(
        [forward_value.reshape(count, chunk, cells), backward_value.reshape(count, chunk, cells), factor_row], axis=1
    )
    gathered = lax.all_to_all(packed, axis, 0, 0, tiled=True)
    block_factor = gathered[:, 2 * chunk, :chunk][:, :, None]
    forward_total = scan_chunks(block_factor, gathered[:, :chunk], False)
    backward_total = scan_chunks(block_factor, gathered[:, chunk : 2 * chunk], True)
    entering = jnp.pad(forward_total[:-1], ((1, 0), (0, 0), (0, 0)))
    arriving = jnp.pad(backward_total[1:], ((0, 1), (0, 0), (0, 0)))
    returned = lax.all_to_all(jnp.concatenate([entering, arriving], axis=1), axis, 0, 0, tiled=True)
    return returned[:, :chunk].reshape(rows, cells), returned[:, chunk:].reshape(rows, cells)


def shift_cells(source, row_shift, col_shift, grid_width):
    cell_count = source.shape[-1]
    margin = grid_width + 1
    padded = jnp.pad(source, [(0, 0)] * (source.ndim - 1) + [(margin, margin)])
    first_cell = margin + row_shift * grid_width + col_shift
    shifted = lax.slice_in_dim(padded, first_cell, first_cell + cell_count, axis=source.ndim - 1)
    column = jnp.arange(cell_count) % grid_width
    inside = (column + col_shift >= 0) & (column + col_shift < grid_width)
    return jnp.where(inside, shifted, jnp.zeros((), source.dtype))


def stencil_stack(source, grid_width, decay_factor):
    parts = [
        shift_cells(source, decay_factor * pair[0], decay_factor * pair[1], grid_width)
        for pair in offsets
    ]
    return jnp.stack(parts, axis=source.ndim - 2)


FRAME_AXES = ("chip", "core")


def pair_then_chip_sum(first, second):
    core = lax.axis_index("core")
    swap = [(0, 1), (1, 0)]
    first_flat, second_flat = first.reshape(-1), second.reshape(-1)
    kept = jnp.where(core == 0, first_flat, second_flat)
    sent = jnp.where(core == 0, second_flat, first_flat)
    pair_sum = (kept + lax.ppermute(sent, "core", swap)).reshape(lax.axis_size("chip"), -1)
    pieces = lax.all_to_all(pair_sum, "chip", 0, 0, tiled=True)
    reduced = jnp.sum(pieces, axis=0, keepdims=True)
    total = lax.all_to_all(jnp.broadcast_to(reduced, pieces.shape), "chip", 0, 0, tiled=True).reshape(-1)
    partner = lax.ppermute(total, "core", swap)
    first_total = jnp.where(core == 0, total, partner)
    second_total = jnp.where(core == 0, partner, total)
    return first_total.reshape(first.shape), second_total.reshape(second.shape)


def body(inputs, decay, kernel_b, kernel_c, cotangent):
    local_rows = kernel_b.shape[1]
    cell_count = inputs.shape[-1]
    blank_state = jnp.zeros((local_rows, cell_count), jnp.float32)
    input_stack = stencil_stack(inputs, W, 1)
    drives = jnp.einsum("kpc,fkcs->fps", kernel_b, input_stack, preferred_element_type=jnp.float32)

    def advance(current, frame_pair):
        frame_rate, drive = frame_pair
        current = frame_rate[:, None] * current + drive
        return (current, current)

    local_end, local_states = lax.scan(advance, blank_state, (decay, drives))
    decay_total = jnp.prod(decay, axis=0)
    cot_stack = stencil_stack(cotangent, W, -1)
    injected = lax.psum_scatter(
        jnp.einsum("kup,fkus->pfs", kernel_c, cot_stack, preferred_element_type=jnp.float32),
        "chan",
        scatter_dimension=0,
        tiled=True,
    )
    injected = jnp.moveaxis(injected, 1, 0)

    def retreat(carried, frame_pair):
        frame_rate, source = frame_pair
        adjoint = source + carried
        return (frame_rate[:, None] * adjoint, adjoint)

    message, local_adjoint = lax.scan(retreat, blank_state, (decay, injected), reverse=True)

    entering, arriving = block_scans(decay_total, local_end, message, FRAME_AXES)
    cumulative = jnp.cumprod(decay, axis=0)
    states = local_states + cumulative[:, :, None] * entering[None]
    previous = jnp.concatenate([entering[None], states[:-1]], axis=0)
    states_bf = states.astype(jnp.bfloat16)
    suffix = jnp.flip(jnp.cumprod(jnp.flip(decay, 0), 0), 0)
    later_decay = jnp.concatenate([suffix[1:], jnp.ones_like(decay[:1])], axis=0)
    adjoint = local_adjoint + later_decay[:, :, None] * arriving[None]
    decay_grad = jnp.sum(adjoint * previous, axis=2)
    adjoint_bf = adjoint.astype(jnp.bfloat16)
    grad_b_part = jnp.einsum(
        "fps,fkcs->kpc", adjoint_bf, input_stack, preferred_element_type=jnp.float32
    )
    shifted = stencil_stack(lax.all_gather(states_bf, "chan", axis=1, tiled=True), W, 1)
    grad_c_part = jnp.einsum(
        "fus,fkps->kup", cotangent, shifted, preferred_element_type=jnp.float32
    )
    grad_b, grad_c = pair_then_chip_sum(grad_b_part, grad_c_part)
    return (grad_b, grad_c, decay_grad)


def solution(mesh):
    chan = mesh.shape["chan"]
    frame_mesh = Mesh(mesh.devices.reshape(-1, 2, chan), (*FRAME_AXES, "chan"))
    in_specs = (
        P(FRAME_AXES, None, None),
        P(FRAME_AXES, "chan"),
        P(None, "chan", None),
        P(None, "chan", None),
        P(FRAME_AXES, "chan", None),
    )
    out_specs = (P(None, "chan", None), P(None, "chan", None), P(FRAME_AXES, "chan"))
    return jax.shard_map(body, mesh=frame_mesh, in_specs=in_specs, out_specs=out_specs, check_vma=False)
```

```python
import jax
import jax.numpy as jnp
from jax import lax
from jax.sharding import Mesh, PartitionSpec as P

W = 64


offsets = ((-1, -1), (-1, 0), (-1, 1), (0, -1), (0, 0), (0, 1), (1, -1), (1, 0), (1, 1))


def passed_along(value, axis, steps):
    count = lax.axis_size(axis)
    first, last = (max(0, -steps), min(count, count - steps))
    return lax.ppermute(value, axis, [(source, source + steps) for source in range(first, last)])


def scan_chunks(factor, value, reverse):
    count = value.shape[0]
    distance = 1
    while distance < count:
        if reverse:
            pads = ((0, distance), (0, 0), (0, 0))
            earlier_value = jnp.pad(value[distance:], pads)
            earlier_factor = jnp.pad(factor[distance:], pads)
        else:
            pads = ((distance, 0), (0, 0), (0, 0))
            earlier_value = jnp.pad(value[:-distance], pads)
            earlier_factor = jnp.pad(factor[:-distance], pads)
        value = value + factor * earlier_value
        factor = factor * earlier_factor
        distance *= 2
    return value


def block_scan(factor, value, axis, reverse):
    count = lax.axis_size(axis)
    rows, cells = value.shape
    chunk = rows // count
    factor_row = jnp.pad(factor.reshape(count, chunk), ((0, 0), (0, cells - chunk)))[:, None, :]
    packed = jnp.concatenate([value.reshape(count, chunk, cells), factor_row], axis=1)
    gathered = lax.all_to_all(packed, axis, 0, 0, tiled=True)
    total = scan_chunks(gathered[:, chunk, :chunk][:, :, None], gathered[:, :chunk], reverse)
    if reverse:
        shifted = jnp.pad(total[1:], ((0, 1), (0, 0), (0, 0)))
    else:
        shifted = jnp.pad(total[:-1], ((1, 0), (0, 0), (0, 0)))
    return lax.all_to_all(shifted, axis, 0, 0, tiled=True).reshape(rows, cells)


def shift_cells(source, row_shift, col_shift, grid_width):
    cell_count = source.shape[-1]
    margin = grid_width + 1
    padded = jnp.pad(source, [(0, 0)] * (source.ndim - 1) + [(margin, margin)])
    first_cell = margin + row_shift * grid_width + col_shift
    shifted = lax.slice_in_dim(padded, first_cell, first_cell + cell_count, axis=source.ndim - 1)
    column = jnp.arange(cell_count) % grid_width
    inside = (column + col_shift >= 0) & (column + col_shift < grid_width)
    return jnp.where(inside, shifted, jnp.zeros((), source.dtype))


def stencil_stack(source, grid_width, decay_factor):
    parts = [
        shift_cells(source, decay_factor * pair[0], decay_factor * pair[1], grid_width)
        for pair in offsets
    ]
    return jnp.stack(parts, axis=source.ndim - 2)


FRAME_AXES = ("chip", "core")


def pair_then_chip_sum(first, second):
    core = lax.axis_index("core")
    swap = [(0, 1), (1, 0)]
    first_flat, second_flat = first.reshape(-1), second.reshape(-1)
    kept = jnp.where(core == 0, first_flat, second_flat)
    sent = jnp.where(core == 0, second_flat, first_flat)
    pair_sum = (kept + lax.ppermute(sent, "core", swap)).reshape(lax.axis_size("chip"), -1)
    pieces = lax.all_to_all(pair_sum, "chip", 0, 0, tiled=True)
    reduced = jnp.sum(pieces, axis=0, keepdims=True)
    total = lax.all_to_all(jnp.broadcast_to(reduced, pieces.shape), "chip", 0, 0, tiled=True).reshape(-1)
    partner = lax.ppermute(total, "core", swap)
    first_total = jnp.where(core == 0, total, partner)
    second_total = jnp.where(core == 0, partner, total)
    return first_total.reshape(first.shape), second_total.reshape(second.shape)


def body(inputs, decay, kernel_b, kernel_c, cotangent):
    local_rows = kernel_b.shape[1]
    cell_count = inputs.shape[-1]
    blank_state = jnp.zeros((local_rows, cell_count), jnp.float32)
    input_stack = stencil_stack(inputs, W, 1)
    drives = jnp.einsum("kpc,fkcs->fps", kernel_b, input_stack, preferred_element_type=jnp.float32)

    def advance(current, frame_pair):
        frame_rate, drive = frame_pair
        current = frame_rate[:, None] * current + drive
        return (current, current)

    local_end, local_states = lax.scan(advance, blank_state, (decay, drives))
    decay_total = jnp.prod(decay, axis=0)
    entering = block_scan(decay_total, local_end, FRAME_AXES, False)
    cot_stack = stencil_stack(cotangent, W, -1)
    injected = lax.psum_scatter(
        jnp.einsum("kup,fkus->pfs", kernel_c, cot_stack, preferred_element_type=jnp.float32),
        "chan",
        scatter_dimension=0,
        tiled=True,
    )
    entering, injected = lax.optimization_barrier((entering, injected))
    injected = jnp.moveaxis(injected, 1, 0)

    def retreat(carried, frame_pair):
        frame_rate, source = frame_pair
        adjoint = source + carried
        return (frame_rate[:, None] * adjoint, adjoint)

    message, local_adjoint = lax.scan(retreat, blank_state, (decay, injected), reverse=True)

    arriving = block_scan(decay_total, message, FRAME_AXES, True)
    cumulative = jnp.cumprod(decay, axis=0)
    states = local_states + cumulative[:, :, None] * entering[None]
    previous = jnp.concatenate([entering[None], states[:-1]], axis=0)
    states_bf = states.astype(jnp.bfloat16)
    suffix = jnp.flip(jnp.cumprod(jnp.flip(decay, 0), 0), 0)
    later_decay = jnp.concatenate([suffix[1:], jnp.ones_like(decay[:1])], axis=0)
    adjoint = local_adjoint + later_decay[:, :, None] * arriving[None]
    decay_grad = jnp.sum(adjoint * previous, axis=2)
    adjoint_bf = adjoint.astype(jnp.bfloat16)
    grad_b_part = jnp.einsum(
        "fps,fkcs->kpc", adjoint_bf, input_stack, preferred_element_type=jnp.float32
    )
    shifted = stencil_stack(lax.all_gather(states_bf, "chan", axis=1, tiled=True), W, 1)
    grad_c_part = jnp.einsum(
        "fus,fkps->kup", cotangent, shifted, preferred_element_type=jnp.float32
    )
    grad_b, grad_c = pair_then_chip_sum(grad_b_part, grad_c_part)
    return (grad_b, grad_c, decay_grad)


def solution(mesh):
    chan = mesh.shape["chan"]
    frame_mesh = Mesh(mesh.devices.reshape(-1, 2, chan), (*FRAME_AXES, "chan"))
    in_specs = (
        P(FRAME_AXES, None, None),
        P(FRAME_AXES, "chan"),
        P(None, "chan", None),
        P(None, "chan", None),
        P(FRAME_AXES, "chan", None),
    )
    out_specs = (P(None, "chan", None), P(None, "chan", None), P(FRAME_AXES, "chan"))
    return jax.shard_map(body, mesh=frame_mesh, in_specs=in_specs, out_specs=out_specs, check_vma=False)
```

```python
import jax
import jax.numpy as jnp
from jax import lax
from jax.sharding import Mesh, PartitionSpec as P

W = 64


offsets = ((-1, -1), (-1, 0), (-1, 1), (0, -1), (0, 0), (0, 1), (1, -1), (1, 0), (1, 1))


def passed_along(value, axis, steps):
    count = lax.axis_size(axis)
    first, last = (max(0, -steps), min(count, count - steps))
    return lax.ppermute(value, axis, [(source, source + steps) for source in range(first, last)])


def scan_chunks(factor, value, reverse):
    count = value.shape[0]
    distance = 1
    while distance < count:
        if reverse:
            pads = ((0, distance), (0, 0), (0, 0))
            earlier_value = jnp.pad(value[distance:], pads)
            earlier_factor = jnp.pad(factor[distance:], pads)
        else:
            pads = ((distance, 0), (0, 0), (0, 0))
            earlier_value = jnp.pad(value[:-distance], pads)
            earlier_factor = jnp.pad(factor[:-distance], pads)
        value = value + factor * earlier_value
        factor = factor * earlier_factor
        distance *= 2
    return value


def pack_chunks(factor, value, count):
    rows, cells = value.shape
    chunk = rows // count
    factor_row = jnp.pad(factor.reshape(count, chunk), ((0, 0), (0, cells - chunk)))[:, None, :]
    return jnp.concatenate([value.reshape(count, chunk, cells), factor_row], axis=1)


def scan_owned(gathered, reverse):
    chunk = gathered.shape[1] - 1
    total = scan_chunks(gathered[:, chunk, :chunk][:, :, None], gathered[:, :chunk], reverse)
    if reverse:
        return jnp.pad(total[1:], ((0, 1), (0, 0), (0, 0)))
    return jnp.pad(total[:-1], ((1, 0), (0, 0), (0, 0)))


def shift_cells(source, row_shift, col_shift, grid_width):
    cell_count = source.shape[-1]
    margin = grid_width + 1
    padded = jnp.pad(source, [(0, 0)] * (source.ndim - 1) + [(margin, margin)])
    first_cell = margin + row_shift * grid_width + col_shift
    shifted = lax.slice_in_dim(padded, first_cell, first_cell + cell_count, axis=source.ndim - 1)
    column = jnp.arange(cell_count) % grid_width
    inside = (column + col_shift >= 0) & (column + col_shift < grid_width)
    return jnp.where(inside, shifted, jnp.zeros((), source.dtype))


def stencil_stack(source, grid_width, decay_factor):
    parts = [
        shift_cells(source, decay_factor * pair[0], decay_factor * pair[1], grid_width)
        for pair in offsets
    ]
    return jnp.stack(parts, axis=source.ndim - 2)


FRAME_AXES = ("chip", "core")


def pair_then_chip_sum(first, second):
    core = lax.axis_index("core")
    swap = [(0, 1), (1, 0)]
    first_flat, second_flat = first.reshape(-1), second.reshape(-1)
    kept = jnp.where(core == 0, first_flat, second_flat)
    sent = jnp.where(core == 0, second_flat, first_flat)
    pair_sum = (kept + lax.ppermute(sent, "core", swap)).reshape(lax.axis_size("chip"), -1)
    pieces = lax.all_to_all(pair_sum, "chip", 0, 0, tiled=True)
    reduced = jnp.sum(pieces, axis=0, keepdims=True)
    total = lax.all_to_all(jnp.broadcast_to(reduced, pieces.shape), "chip", 0, 0, tiled=True).reshape(-1)
    partner = lax.ppermute(total, "core", swap)
    first_total = jnp.where(core == 0, total, partner)
    second_total = jnp.where(core == 0, partner, total)
    return first_total.reshape(first.shape), second_total.reshape(second.shape)


def body(inputs, decay, kernel_b, kernel_c, cotangent):
    local_rows = kernel_b.shape[1]
    cell_count = inputs.shape[-1]
    blank_state = jnp.zeros((local_rows, cell_count), jnp.float32)
    input_stack = stencil_stack(inputs, W, 1)
    drives = jnp.einsum("kpc,fkcs->fps", kernel_b, input_stack, preferred_element_type=jnp.float32)

    def advance(current, frame_pair):
        frame_rate, drive = frame_pair
        current = frame_rate[:, None] * current + drive
        return (current, current)

    local_end, local_states = lax.scan(advance, blank_state, (decay, drives))
    decay_total = jnp.prod(decay, axis=0)
    blocks = lax.axis_size(FRAME_AXES)
    rows = local_end.shape[0]
    chunk = rows // blocks
    entering_owned = scan_owned(lax.all_to_all(pack_chunks(decay_total, local_end, blocks), FRAME_AXES, 0, 0, tiled=True), False)
    cot_stack = stencil_stack(cotangent, W, -1)
    injected = lax.psum_scatter(
        jnp.einsum("kup,fkus->pfs", kernel_c, cot_stack, preferred_element_type=jnp.float32),
        "chan",
        scatter_dimension=0,
        tiled=True,
    )
    entering_owned, injected = lax.optimization_barrier((entering_owned, injected))
    injected = jnp.moveaxis(injected, 1, 0)

    def retreat(carried, frame_pair):
        frame_rate, source = frame_pair
        adjoint = source + carried
        return (frame_rate[:, None] * adjoint, adjoint)

    message, local_adjoint = lax.scan(retreat, blank_state, (decay, injected), reverse=True)

    exchanged = lax.all_to_all(
        jnp.concatenate([entering_owned, pack_chunks(decay_total, message, blocks)], axis=1), FRAME_AXES, 0, 0, tiled=True
    )
    entering = exchanged[:, :chunk].reshape(rows, cell_count)
    arriving_owned = scan_owned(exchanged[:, chunk:], True)
    arriving = lax.all_to_all(arriving_owned, FRAME_AXES, 0, 0, tiled=True).reshape(rows, cell_count)
    cumulative = jnp.cumprod(decay, axis=0)
    states = local_states + cumulative[:, :, None] * entering[None]
    previous = jnp.concatenate([entering[None], states[:-1]], axis=0)
    states_bf = states.astype(jnp.bfloat16)
    suffix = jnp.flip(jnp.cumprod(jnp.flip(decay, 0), 0), 0)
    later_decay = jnp.concatenate([suffix[1:], jnp.ones_like(decay[:1])], axis=0)
    adjoint = local_adjoint + later_decay[:, :, None] * arriving[None]
    decay_grad = jnp.sum(adjoint * previous, axis=2)
    adjoint_bf = adjoint.astype(jnp.bfloat16)
    grad_b_part = jnp.einsum(
        "fps,fkcs->kpc", adjoint_bf, input_stack, preferred_element_type=jnp.float32
    )
    shifted = stencil_stack(lax.all_gather(states_bf, "chan", axis=1, tiled=True), W, 1)
    grad_c_part = jnp.einsum(
        "fus,fkps->kup", cotangent, shifted, preferred_element_type=jnp.float32
    )
    grad_b, grad_c = pair_then_chip_sum(grad_b_part, grad_c_part)
    return (grad_b, grad_c, decay_grad)


def solution(mesh):
    chan = mesh.shape["chan"]
    frame_mesh = Mesh(mesh.devices.reshape(-1, 2, chan), (*FRAME_AXES, "chan"))
    in_specs = (
        P(FRAME_AXES, None, None),
        P(FRAME_AXES, "chan"),
        P(None, "chan", None),
        P(None, "chan", None),
        P(FRAME_AXES, "chan", None),
    )
    out_specs = (P(None, "chan", None), P(None, "chan", None), P(FRAME_AXES, "chan"))
    return jax.shard_map(body, mesh=frame_mesh, in_specs=in_specs, out_specs=out_specs, check_vma=False)
```

```python
import jax
import jax.numpy as jnp
from jax import lax
from jax.sharding import Mesh, PartitionSpec as P

W = 64


offsets = ((-1, -1), (-1, 0), (-1, 1), (0, -1), (0, 0), (0, 1), (1, -1), (1, 0), (1, 1))


def passed_along(value, axis, steps):
    count = lax.axis_size(axis)
    first, last = (max(0, -steps), min(count, count - steps))
    return lax.ppermute(value, axis, [(source, source + steps) for source in range(first, last)])


def scan_chunks(factor, value, reverse):
    count = value.shape[0]
    distance = 1
    while distance < count:
        if reverse:
            pads = ((0, distance), (0, 0), (0, 0))
            earlier_value = jnp.pad(value[distance:], pads)
            earlier_factor = jnp.pad(factor[distance:], pads)
        else:
            pads = ((distance, 0), (0, 0), (0, 0))
            earlier_value = jnp.pad(value[:-distance], pads)
            earlier_factor = jnp.pad(factor[:-distance], pads)
        value = value + factor * earlier_value
        factor = factor * earlier_factor
        distance *= 2
    return value


def pack_chunks(factor, value, count):
    rows, cells = value.shape
    chunk = rows // count
    factor_row = jnp.pad(factor.reshape(count, chunk), ((0, 0), (0, cells - chunk)))[:, None, :]
    return jnp.concatenate([value.reshape(count, chunk, cells), factor_row], axis=1)


def scan_owned(gathered, reverse):
    chunk = gathered.shape[1] - 1
    total = scan_chunks(gathered[:, chunk, :chunk][:, :, None], gathered[:, :chunk], reverse)
    if reverse:
        return jnp.pad(total[1:], ((0, 1), (0, 0), (0, 0)))
    return jnp.pad(total[:-1], ((1, 0), (0, 0), (0, 0)))


def shift_cells(source, row_shift, col_shift, grid_width):
    cell_count = source.shape[-1]
    margin = grid_width + 1
    padded = jnp.pad(source, [(0, 0)] * (source.ndim - 1) + [(margin, margin)])
    first_cell = margin + row_shift * grid_width + col_shift
    shifted = lax.slice_in_dim(padded, first_cell, first_cell + cell_count, axis=source.ndim - 1)
    column = jnp.arange(cell_count) % grid_width
    inside = (column + col_shift >= 0) & (column + col_shift < grid_width)
    return jnp.where(inside, shifted, jnp.zeros((), source.dtype))


def stencil_stack(source, grid_width, decay_factor):
    parts = [
        shift_cells(source, decay_factor * pair[0], decay_factor * pair[1], grid_width)
        for pair in offsets
    ]
    return jnp.stack(parts, axis=source.ndim - 2)


def stencil_conv(inputs, kernel, width):
    frames, chans, cells = inputs.shape
    image = inputs.reshape(frames, chans, cells // width, width)
    taps = kernel.reshape(3, 3, kernel.shape[1], chans).transpose(2, 3, 0, 1)
    out = lax.conv_general_dilated(
        image, taps, (1, 1), ((1, 1), (1, 1)), dimension_numbers=("NCHW", "OIHW", "NCHW"),
        preferred_element_type=jnp.float32,
    )
    return out.reshape(frames, kernel.shape[1], cells)


FRAME_AXES = ("chip", "core")


def pair_then_chip_sum(first, second):
    core = lax.axis_index("core")
    swap = [(0, 1), (1, 0)]
    first_flat, second_flat = first.reshape(-1), second.reshape(-1)
    kept = jnp.where(core == 0, first_flat, second_flat)
    sent = jnp.where(core == 0, second_flat, first_flat)
    pair_sum = (kept + lax.ppermute(sent, "core", swap)).reshape(lax.axis_size("chip"), -1)
    pieces = lax.all_to_all(pair_sum, "chip", 0, 0, tiled=True)
    reduced = jnp.sum(pieces, axis=0, keepdims=True)
    total = lax.all_to_all(jnp.broadcast_to(reduced, pieces.shape), "chip", 0, 0, tiled=True).reshape(-1)
    partner = lax.ppermute(total, "core", swap)
    first_total = jnp.where(core == 0, total, partner)
    second_total = jnp.where(core == 0, partner, total)
    return first_total.reshape(first.shape), second_total.reshape(second.shape)


def body(inputs, decay, kernel_b, kernel_c, cotangent):
    local_rows = kernel_b.shape[1]
    cell_count = inputs.shape[-1]
    blank_state = jnp.zeros((local_rows, cell_count), jnp.float32)
    drives = stencil_conv(inputs, kernel_b, W)

    def advance(current, frame_pair):
        frame_rate, drive = frame_pair
        current = frame_rate[:, None] * current + drive
        return (current, current)

    local_end, local_states = lax.scan(advance, blank_state, (decay, drives))
    decay_total = jnp.prod(decay, axis=0)
    blocks = lax.axis_size(FRAME_AXES)
    rows = local_end.shape[0]
    chunk = rows // blocks
    entering_owned = scan_owned(lax.all_to_all(pack_chunks(decay_total, local_end, blocks), FRAME_AXES, 0, 0, tiled=True), False)
    cot_stack = stencil_stack(cotangent, W, -1)
    injected = lax.psum_scatter(
        jnp.einsum("kup,fkus->pfs", kernel_c, cot_stack, preferred_element_type=jnp.float32),
        "chan",
        scatter_dimension=0,
        tiled=True,
    )
    entering_owned, injected = lax.optimization_barrier((entering_owned, injected))
    injected = jnp.moveaxis(injected, 1, 0)

    def retreat(carried, frame_pair):
        frame_rate, source = frame_pair
        adjoint = source + carried
        return (frame_rate[:, None] * adjoint, adjoint)

    message, local_adjoint = lax.scan(retreat, blank_state, (decay, injected), reverse=True)

    exchanged = lax.all_to_all(
        jnp.concatenate([entering_owned, pack_chunks(decay_total, message, blocks)], axis=1), FRAME_AXES, 0, 0, tiled=True
    )
    entering = exchanged[:, :chunk].reshape(rows, cell_count)
    arriving_owned = scan_owned(exchanged[:, chunk:], True)
    arriving = lax.all_to_all(arriving_owned, FRAME_AXES, 0, 0, tiled=True).reshape(rows, cell_count)
    cumulative = jnp.cumprod(decay, axis=0)
    states = local_states + cumulative[:, :, None] * entering[None]
    previous = jnp.concatenate([entering[None], states[:-1]], axis=0)
    states_bf = states.astype(jnp.bfloat16)
    suffix = jnp.flip(jnp.cumprod(jnp.flip(decay, 0), 0), 0)
    later_decay = jnp.concatenate([suffix[1:], jnp.ones_like(decay[:1])], axis=0)
    adjoint = local_adjoint + later_decay[:, :, None] * arriving[None]
    decay_grad = jnp.sum(adjoint * previous, axis=2)
    adjoint_bf = adjoint.astype(jnp.bfloat16)
    input_stack = stencil_stack(inputs, W, 1)
    grad_b_part = jnp.einsum(
        "fps,fkcs->kpc", adjoint_bf, input_stack, preferred_element_type=jnp.float32
    )
    all_states = lax.all_gather(states_bf, "chan", axis=1, tiled=True)
    grad_c_part = jnp.einsum(
        "fkus,fps->kup", cot_stack, all_states, preferred_element_type=jnp.float32
    )
    grad_b, grad_c = pair_then_chip_sum(grad_b_part, grad_c_part)
    return (grad_b, grad_c, decay_grad)


def solution(mesh):
    chan = mesh.shape["chan"]
    frame_mesh = Mesh(mesh.devices.reshape(-1, 2, chan), (*FRAME_AXES, "chan"))
    in_specs = (
        P(FRAME_AXES, None, None),
        P(FRAME_AXES, "chan"),
        P(None, "chan", None),
        P(None, "chan", None),
        P(FRAME_AXES, "chan", None),
    )
    out_specs = (P(None, "chan", None), P(None, "chan", None), P(FRAME_AXES, "chan"))
    return jax.shard_map(body, mesh=frame_mesh, in_specs=in_specs, out_specs=out_specs, check_vma=False)
```

```python
import jax
import jax.numpy as jnp
from jax import lax
from jax.sharding import Mesh, PartitionSpec as P

W = 64


offsets = ((-1, -1), (-1, 0), (-1, 1), (0, -1), (0, 0), (0, 1), (1, -1), (1, 0), (1, 1))


def passed_along(value, axis, steps):
    count = lax.axis_size(axis)
    first, last = (max(0, -steps), min(count, count - steps))
    return lax.ppermute(value, axis, [(source, source + steps) for source in range(first, last)])


def scan_chunks(factor, value, reverse):
    count = value.shape[0]
    distance = 1
    while distance < count:
        if reverse:
            pads = ((0, distance), (0, 0), (0, 0))
            earlier_value = jnp.pad(value[distance:], pads)
            earlier_factor = jnp.pad(factor[distance:], pads)
        else:
            pads = ((distance, 0), (0, 0), (0, 0))
            earlier_value = jnp.pad(value[:-distance], pads)
            earlier_factor = jnp.pad(factor[:-distance], pads)
        value = value + factor * earlier_value
        factor = factor * earlier_factor
        distance *= 2
    return value


def pack_chunks(factor, value, count):
    rows, cells = value.shape
    chunk = rows // count
    factor_row = jnp.pad(factor.reshape(count, chunk), ((0, 0), (0, cells - chunk)))[:, None, :]
    return jnp.concatenate([value.reshape(count, chunk, cells), factor_row], axis=1)


def scan_owned(gathered, reverse):
    chunk = gathered.shape[1] - 1
    total = scan_chunks(gathered[:, chunk, :chunk][:, :, None], gathered[:, :chunk], reverse)
    if reverse:
        return jnp.pad(total[1:], ((0, 1), (0, 0), (0, 0)))
    return jnp.pad(total[:-1], ((1, 0), (0, 0), (0, 0)))


def shift_cells(source, row_shift, col_shift, grid_width):
    cell_count = source.shape[-1]
    margin = grid_width + 1
    padded = jnp.pad(source, [(0, 0)] * (source.ndim - 1) + [(margin, margin)])
    first_cell = margin + row_shift * grid_width + col_shift
    shifted = lax.slice_in_dim(padded, first_cell, first_cell + cell_count, axis=source.ndim - 1)
    column = jnp.arange(cell_count) % grid_width
    inside = (column + col_shift >= 0) & (column + col_shift < grid_width)
    return jnp.where(inside, shifted, jnp.zeros((), source.dtype))


def stencil_stack(source, grid_width, decay_factor):
    parts = [
        shift_cells(source, decay_factor * pair[0], decay_factor * pair[1], grid_width)
        for pair in offsets
    ]
    return jnp.stack(parts, axis=source.ndim - 2)


def stencil_conv(inputs, kernel, width):
    frames, chans, cells = inputs.shape
    image = inputs.reshape(frames, chans, cells // width, width)
    taps = kernel.reshape(3, 3, kernel.shape[1], chans).transpose(2, 3, 0, 1)
    out = lax.conv_general_dilated(
        image, taps, (1, 1), ((1, 1), (1, 1)), dimension_numbers=("NCHW", "OIHW", "NCHW"),
        preferred_element_type=jnp.float32,
    )
    return out.reshape(frames, kernel.shape[1], cells)


FRAME_AXES = ("chip", "core")


def pair_then_chip_sum(first, second):
    core = lax.axis_index("core")
    swap = [(0, 1), (1, 0)]
    first_flat, second_flat = first.reshape(-1), second.reshape(-1)
    kept = jnp.where(core == 0, first_flat, second_flat)
    sent = jnp.where(core == 0, second_flat, first_flat)
    pair_sum = (kept + lax.ppermute(sent, "core", swap)).reshape(lax.axis_size("chip"), -1)
    pieces = lax.all_to_all(pair_sum, "chip", 0, 0, tiled=True)
    reduced = jnp.sum(pieces, axis=0, keepdims=True)
    total = lax.all_to_all(jnp.broadcast_to(reduced, pieces.shape), "chip", 0, 0, tiled=True).reshape(-1)
    partner = lax.ppermute(total, "core", swap)
    first_total = jnp.where(core == 0, total, partner)
    second_total = jnp.where(core == 0, partner, total)
    return first_total.reshape(first.shape), second_total.reshape(second.shape)


def body(inputs, decay, kernel_b, kernel_c, cotangent):
    local_rows = kernel_b.shape[1]
    cell_count = inputs.shape[-1]
    blank_state = jnp.zeros((local_rows, cell_count), jnp.float32)
    drives = stencil_conv(inputs, kernel_b, W)

    def advance(current, frame_pair):
        frame_rate, drive = frame_pair
        current = frame_rate[:, None] * current + drive
        return (current, current)

    local_end, local_states = lax.scan(advance, blank_state, (decay, drives))
    decay_total = jnp.prod(decay, axis=0)
    blocks = lax.axis_size(FRAME_AXES)
    rows = local_end.shape[0]
    chunk = rows // blocks
    entering_owned = scan_owned(lax.all_to_all(pack_chunks(decay_total, local_end, blocks), FRAME_AXES, 0, 0, tiled=True), False)
    cot_stack = stencil_stack(cotangent, W, -1)
    all_cotangent = lax.all_gather(cotangent, "chan", axis=1, tiled=True)
    readout_local = lax.all_to_all(kernel_c, "chan", 2, 1, tiled=True)
    injected = stencil_conv(all_cotangent, jnp.flip(readout_local, 0).transpose(0, 2, 1), W)
    entering_owned, injected = lax.optimization_barrier((entering_owned, injected))

    def retreat(carried, frame_pair):
        frame_rate, source = frame_pair
        adjoint = source + carried
        return (frame_rate[:, None] * adjoint, adjoint)

    message, local_adjoint = lax.scan(retreat, blank_state, (decay, injected), reverse=True)

    exchanged = lax.all_to_all(
        jnp.concatenate([entering_owned, pack_chunks(decay_total, message, blocks)], axis=1), FRAME_AXES, 0, 0, tiled=True
    )
    entering = exchanged[:, :chunk].reshape(rows, cell_count)
    arriving_owned = scan_owned(exchanged[:, chunk:], True)
    arriving = lax.all_to_all(arriving_owned, FRAME_AXES, 0, 0, tiled=True).reshape(rows, cell_count)
    cumulative = jnp.cumprod(decay, axis=0)
    states = local_states + cumulative[:, :, None] * entering[None]
    previous = jnp.concatenate([entering[None], states[:-1]], axis=0)
    states_bf = states.astype(jnp.bfloat16)
    suffix = jnp.flip(jnp.cumprod(jnp.flip(decay, 0), 0), 0)
    later_decay = jnp.concatenate([suffix[1:], jnp.ones_like(decay[:1])], axis=0)
    adjoint = local_adjoint + later_decay[:, :, None] * arriving[None]
    decay_grad = jnp.sum(adjoint * previous, axis=2)
    adjoint_bf = adjoint.astype(jnp.bfloat16)
    input_stack = stencil_stack(inputs, W, 1)
    grad_b_part = jnp.einsum(
        "fps,fkcs->kpc", adjoint_bf, input_stack, preferred_element_type=jnp.float32
    )
    all_states = lax.all_gather(states_bf, "chan", axis=1, tiled=True)
    grad_c_part = jnp.einsum(
        "fkus,fps->kup", cot_stack, all_states, preferred_element_type=jnp.float32
    )
    grad_b, grad_c = pair_then_chip_sum(grad_b_part, grad_c_part)
    return (grad_b, grad_c, decay_grad)


def solution(mesh):
    chan = mesh.shape["chan"]
    frame_mesh = Mesh(mesh.devices.reshape(-1, 2, chan), (*FRAME_AXES, "chan"))
    in_specs = (
        P(FRAME_AXES, None, None),
        P(FRAME_AXES, "chan"),
        P(None, "chan", None),
        P(None, "chan", None),
        P(FRAME_AXES, "chan", None),
    )
    out_specs = (P(None, "chan", None), P(None, "chan", None), P(FRAME_AXES, "chan"))
    return jax.shard_map(body, mesh=frame_mesh, in_specs=in_specs, out_specs=out_specs, check_vma=False)
```

```python
import jax
import jax.numpy as jnp
from jax import lax
from jax.sharding import Mesh, PartitionSpec as P

W = 64


offsets = ((-1, -1), (-1, 0), (-1, 1), (0, -1), (0, 0), (0, 1), (1, -1), (1, 0), (1, 1))


def passed_along(value, axis, steps):
    count = lax.axis_size(axis)
    first, last = (max(0, -steps), min(count, count - steps))
    return lax.ppermute(value, axis, [(source, source + steps) for source in range(first, last)])


def scan_chunks(factor, value, reverse):
    count = value.shape[0]
    distance = 1
    while distance < count:
        if reverse:
            pads = ((0, distance), (0, 0), (0, 0))
            earlier_value = jnp.pad(value[distance:], pads)
            earlier_factor = jnp.pad(factor[distance:], pads)
        else:
            pads = ((distance, 0), (0, 0), (0, 0))
            earlier_value = jnp.pad(value[:-distance], pads)
            earlier_factor = jnp.pad(factor[:-distance], pads)
        value = value + factor * earlier_value
        factor = factor * earlier_factor
        distance *= 2
    return value


def pack_chunks(factor, value, count):
    rows, cells = value.shape
    chunk = rows // count
    factor_row = jnp.pad(factor.reshape(count, chunk), ((0, 0), (0, cells - chunk)))[:, None, :]
    return jnp.concatenate([value.reshape(count, chunk, cells), factor_row], axis=1)


def scan_owned(gathered, reverse):
    chunk = gathered.shape[1] - 1
    total = scan_chunks(gathered[:, chunk, :chunk][:, :, None], gathered[:, :chunk], reverse)
    if reverse:
        return jnp.pad(total[1:], ((0, 1), (0, 0), (0, 0)))
    return jnp.pad(total[:-1], ((1, 0), (0, 0), (0, 0)))


def shift_cells(source, row_shift, col_shift, grid_width):
    cell_count = source.shape[-1]
    margin = grid_width + 1
    padded = jnp.pad(source, [(0, 0)] * (source.ndim - 1) + [(margin, margin)])
    first_cell = margin + row_shift * grid_width + col_shift
    shifted = lax.slice_in_dim(padded, first_cell, first_cell + cell_count, axis=source.ndim - 1)
    column = jnp.arange(cell_count) % grid_width
    inside = (column + col_shift >= 0) & (column + col_shift < grid_width)
    return jnp.where(inside, shifted, jnp.zeros((), source.dtype))


def stencil_stack(source, grid_width, decay_factor):
    parts = [
        shift_cells(source, decay_factor * pair[0], decay_factor * pair[1], grid_width)
        for pair in offsets
    ]
    return jnp.stack(parts, axis=source.ndim - 2)


def stencil_conv(inputs, kernel, width):
    frames, chans, cells = inputs.shape
    image = inputs.reshape(frames, chans, cells // width, width)
    taps = kernel.reshape(3, 3, kernel.shape[1], chans).transpose(2, 3, 0, 1)
    out = lax.conv_general_dilated(
        image, taps, (1, 1), ((1, 1), (1, 1)), dimension_numbers=("NCHW", "OIHW", "NCHW"),
        preferred_element_type=jnp.float32,
    )
    return out.reshape(frames, kernel.shape[1], cells)


FRAME_AXES = ("chip", "core")


def pair_then_chip_sum(first, second):
    core = lax.axis_index("core")
    chips = lax.axis_size("chip")
    swap = [(0, 1), (1, 0)]
    shape = (chips, first.size // (chips * first.shape[-1]), first.shape[-1])
    first_rows, second_rows = first.reshape(shape), second.reshape(shape)
    kept = jnp.where(core == 0, first_rows, second_rows)
    sent = jnp.where(core == 0, second_rows, first_rows)
    pair_sum = kept + lax.ppermute(sent, "core", swap)
    pieces = lax.all_to_all(pair_sum, "chip", 0, 0, tiled=True)
    reduced = jnp.sum(pieces, axis=0, keepdims=True)
    total = lax.all_to_all(jnp.broadcast_to(reduced, pieces.shape), "chip", 0, 0, tiled=True)
    partner = lax.ppermute(total, "core", swap)
    first_total = jnp.where(core == 0, total, partner)
    second_total = jnp.where(core == 0, partner, total)
    return first_total.reshape(first.shape), second_total.reshape(second.shape)


def body(inputs, decay, kernel_b, kernel_c, cotangent):
    local_rows = kernel_b.shape[1]
    cell_count = inputs.shape[-1]
    blank_state = jnp.zeros((local_rows, cell_count), jnp.float32)
    drives = stencil_conv(inputs, kernel_b, W)

    def advance(current, frame_pair):
        frame_rate, drive = frame_pair
        current = frame_rate[:, None] * current + drive
        return (current, current)

    local_end, local_states = lax.scan(advance, blank_state, (decay, drives))
    decay_total = jnp.prod(decay, axis=0)
    blocks = lax.axis_size(FRAME_AXES)
    rows = local_end.shape[0]
    chunk = rows // blocks
    entering_owned = scan_owned(lax.all_to_all(pack_chunks(decay_total, local_end, blocks), FRAME_AXES, 0, 0, tiled=True), False)
    cot_stack = stencil_stack(cotangent, W, -1)
    injected = lax.psum_scatter(
        jnp.einsum("kup,fkus->pfs", kernel_c, cot_stack, preferred_element_type=jnp.float32),
        "chan",
        scatter_dimension=0,
        tiled=True,
    )
    entering_owned, injected = lax.optimization_barrier((entering_owned, injected))
    injected = jnp.moveaxis(injected, 1, 0)

    def retreat(carried, frame_pair):
        frame_rate, source = frame_pair
        adjoint = source + carried
        return (frame_rate[:, None] * adjoint, adjoint)

    message, local_adjoint = lax.scan(retreat, blank_state, (decay, injected), reverse=True)

    exchanged = lax.all_to_all(
        jnp.concatenate([entering_owned, pack_chunks(decay_total, message, blocks)], axis=1), FRAME_AXES, 0, 0, tiled=True
    )
    entering = exchanged[:, :chunk].reshape(rows, cell_count)
    arriving_owned = scan_owned(exchanged[:, chunk:], True)
    arriving = lax.all_to_all(arriving_owned, FRAME_AXES, 0, 0, tiled=True).reshape(rows, cell_count)
    cumulative = jnp.cumprod(decay, axis=0)
    states = local_states + cumulative[:, :, None] * entering[None]
    previous = jnp.concatenate([entering[None], states[:-1]], axis=0)
    states_bf = states.astype(jnp.bfloat16)
    suffix = jnp.flip(jnp.cumprod(jnp.flip(decay, 0), 0), 0)
    later_decay = jnp.concatenate([suffix[1:], jnp.ones_like(decay[:1])], axis=0)
    adjoint = local_adjoint + later_decay[:, :, None] * arriving[None]
    decay_grad = jnp.sum(adjoint * previous, axis=2)
    adjoint_bf = adjoint.astype(jnp.bfloat16)
    input_stack = stencil_stack(inputs, W, 1)
    grad_b_part = jnp.einsum(
        "fps,fkcs->kpc", adjoint_bf, input_stack, preferred_element_type=jnp.float32
    )
    all_states = lax.all_gather(states_bf, "chan", axis=1, tiled=True)
    grad_c_part = jnp.einsum(
        "fkus,fps->kup", cot_stack, all_states, preferred_element_type=jnp.float32
    )
    grad_b, grad_c = pair_then_chip_sum(grad_b_part, grad_c_part)
    return (grad_b, grad_c, decay_grad)


def solution(mesh):
    chan = mesh.shape["chan"]
    frame_mesh = Mesh(mesh.devices.reshape(-1, 2, chan), (*FRAME_AXES, "chan"))
    in_specs = (
        P(FRAME_AXES, None, None),
        P(FRAME_AXES, "chan"),
        P(None, "chan", None),
        P(None, "chan", None),
        P(FRAME_AXES, "chan", None),
    )
    out_specs = (P(None, "chan", None), P(None, "chan", None), P(FRAME_AXES, "chan"))
    return jax.shard_map(body, mesh=frame_mesh, in_specs=in_specs, out_specs=out_specs, check_vma=False)
```

```python
import jax
import jax.numpy as jnp
from jax import lax
from jax.sharding import Mesh, PartitionSpec as P

W = 64


offsets = ((-1, -1), (-1, 0), (-1, 1), (0, -1), (0, 0), (0, 1), (1, -1), (1, 0), (1, 1))


def passed_along(value, axis, steps):
    count = lax.axis_size(axis)
    first, last = (max(0, -steps), min(count, count - steps))
    return lax.ppermute(value, axis, [(source, source + steps) for source in range(first, last)])


def scan_chunks(factor, value, reverse):
    count = value.shape[0]
    distance = 1
    while distance < count:
        if reverse:
            pads = ((0, distance), (0, 0), (0, 0))
            earlier_value = jnp.pad(value[distance:], pads)
            earlier_factor = jnp.pad(factor[distance:], pads)
        else:
            pads = ((distance, 0), (0, 0), (0, 0))
            earlier_value = jnp.pad(value[:-distance], pads)
            earlier_factor = jnp.pad(factor[:-distance], pads)
        value = value + factor * earlier_value
        factor = factor * earlier_factor
        distance *= 2
    return value


def pack_chunks(factor, value, count):
    rows, cells = value.shape
    chunk = rows // count
    factor_row = jnp.pad(factor.reshape(count, chunk), ((0, 0), (0, cells - chunk)))[:, None, :]
    return jnp.concatenate([value.reshape(count, chunk, cells), factor_row], axis=1)


def scan_owned(gathered, reverse):
    chunk = gathered.shape[1] - 1
    total = scan_chunks(gathered[:, chunk, :chunk][:, :, None], gathered[:, :chunk], reverse)
    if reverse:
        return jnp.pad(total[1:], ((0, 1), (0, 0), (0, 0)))
    return jnp.pad(total[:-1], ((1, 0), (0, 0), (0, 0)))


def shift_cells(source, row_shift, col_shift, grid_width):
    cell_count = source.shape[-1]
    margin = grid_width + 1
    padded = jnp.pad(source, [(0, 0)] * (source.ndim - 1) + [(margin, margin)])
    first_cell = margin + row_shift * grid_width + col_shift
    shifted = lax.slice_in_dim(padded, first_cell, first_cell + cell_count, axis=source.ndim - 1)
    column = jnp.arange(cell_count) % grid_width
    inside = (column + col_shift >= 0) & (column + col_shift < grid_width)
    return jnp.where(inside, shifted, jnp.zeros((), source.dtype))


def stencil_stack(source, grid_width, decay_factor):
    parts = [
        shift_cells(source, decay_factor * pair[0], decay_factor * pair[1], grid_width)
        for pair in offsets
    ]
    return jnp.stack(parts, axis=source.ndim - 2)


def stencil_conv(inputs, kernel, width):
    frames, chans, cells = inputs.shape
    image = inputs.reshape(frames, chans, cells // width, width)
    taps = kernel.reshape(3, 3, kernel.shape[1], chans).transpose(2, 3, 0, 1)
    out = lax.conv_general_dilated(
        image, taps, (1, 1), ((1, 1), (1, 1)), dimension_numbers=("NCHW", "OIHW", "NCHW"),
        preferred_element_type=jnp.float32,
    )
    return out.reshape(frames, kernel.shape[1], cells)


def gather_by_all_to_all(value, axis):
    count = lax.axis_size(axis)
    copies = jnp.broadcast_to(value[None], (count, *value.shape))
    blocks = jnp.moveaxis(lax.all_to_all(copies, axis, 0, 0, tiled=True), 0, 1)
    return blocks.reshape(value.shape[0], count * value.shape[1], *value.shape[2:])


FRAME_AXES = ("chip", "core")


def pair_then_chip_sum(first, second):
    core = lax.axis_index("core")
    swap = [(0, 1), (1, 0)]
    first_flat, second_flat = first.reshape(-1), second.reshape(-1)
    kept = jnp.where(core == 0, first_flat, second_flat)
    sent = jnp.where(core == 0, second_flat, first_flat)
    pair_sum = (kept + lax.ppermute(sent, "core", swap)).reshape(lax.axis_size("chip"), -1)
    pieces = lax.all_to_all(pair_sum, "chip", 0, 0, tiled=True)
    reduced = jnp.sum(pieces, axis=0, keepdims=True)
    total = lax.all_to_all(jnp.broadcast_to(reduced, pieces.shape), "chip", 0, 0, tiled=True).reshape(-1)
    partner = lax.ppermute(total, "core", swap)
    first_total = jnp.where(core == 0, total, partner)
    second_total = jnp.where(core == 0, partner, total)
    return first_total.reshape(first.shape), second_total.reshape(second.shape)


def body(inputs, decay, kernel_b, kernel_c, cotangent):
    local_rows = kernel_b.shape[1]
    cell_count = inputs.shape[-1]
    blank_state = jnp.zeros((local_rows, cell_count), jnp.float32)
    drives = stencil_conv(inputs, kernel_b, W)

    def advance(current, frame_pair):
        frame_rate, drive = frame_pair
        current = frame_rate[:, None] * current + drive
        return (current, current)

    local_end, local_states = lax.scan(advance, blank_state, (decay, drives))
    decay_total = jnp.prod(decay, axis=0)
    blocks = lax.axis_size(FRAME_AXES)
    rows = local_end.shape[0]
    chunk = rows // blocks
    entering_owned = scan_owned(lax.all_to_all(pack_chunks(decay_total, local_end, blocks), FRAME_AXES, 0, 0, tiled=True), False)
    cot_stack = stencil_stack(cotangent, W, -1)
    chans = lax.axis_size("chan")
    taps, outs, states_local = kernel_c.shape[0], kernel_c.shape[1], kernel_b.shape[1]
    readout_blocks = jnp.moveaxis(kernel_c.reshape(taps, outs, chans, states_local), 2, 0)
    readout_local = lax.all_to_all(readout_blocks, "chan", 0, 0, tiled=True)
    readout_local = readout_local.transpose(1, 3, 0, 2).reshape(taps, states_local, chans * outs)
    all_cotangent = gather_by_all_to_all(cotangent, "chan")
    injected = stencil_conv(all_cotangent, jnp.flip(readout_local, 0), W)
    entering_owned, injected = lax.optimization_barrier((entering_owned, injected))

    def retreat(carried, frame_pair):
        frame_rate, source = frame_pair
        adjoint = source + carried
        return (frame_rate[:, None] * adjoint, adjoint)

    message, local_adjoint = lax.scan(retreat, blank_state, (decay, injected), reverse=True)

    exchanged = lax.all_to_all(
        jnp.concatenate([entering_owned, pack_chunks(decay_total, message, blocks)], axis=1), FRAME_AXES, 0, 0, tiled=True
    )
    entering = exchanged[:, :chunk].reshape(rows, cell_count)
    arriving_owned = scan_owned(exchanged[:, chunk:], True)
    arriving = lax.all_to_all(arriving_owned, FRAME_AXES, 0, 0, tiled=True).reshape(rows, cell_count)
    cumulative = jnp.cumprod(decay, axis=0)
    states = local_states + cumulative[:, :, None] * entering[None]
    previous = jnp.concatenate([entering[None], states[:-1]], axis=0)
    states_bf = states.astype(jnp.bfloat16)
    suffix = jnp.flip(jnp.cumprod(jnp.flip(decay, 0), 0), 0)
    later_decay = jnp.concatenate([suffix[1:], jnp.ones_like(decay[:1])], axis=0)
    adjoint = local_adjoint + later_decay[:, :, None] * arriving[None]
    decay_grad = jnp.sum(adjoint * previous, axis=2)
    adjoint_bf = adjoint.astype(jnp.bfloat16)
    input_stack = stencil_stack(inputs, W, 1)
    grad_b_part = jnp.einsum(
        "fps,fkcs->kpc", adjoint_bf, input_stack, preferred_element_type=jnp.float32
    )
    all_states = gather_by_all_to_all(states_bf, "chan")
    grad_c_part = jnp.einsum(
        "fkus,fps->kup", cot_stack, all_states, preferred_element_type=jnp.float32
    )
    grad_b, grad_c = pair_then_chip_sum(grad_b_part, grad_c_part)
    return (grad_b, grad_c, decay_grad)


def solution(mesh):
    chan = mesh.shape["chan"]
    frame_mesh = Mesh(mesh.devices.reshape(-1, 2, chan), (*FRAME_AXES, "chan"))
    in_specs = (
        P(FRAME_AXES, None, None),
        P(FRAME_AXES, "chan"),
        P(None, "chan", None),
        P(None, "chan", None),
        P(FRAME_AXES, "chan", None),
    )
    out_specs = (P(None, "chan", None), P(None, "chan", None), P(FRAME_AXES, "chan"))
    return jax.shard_map(body, mesh=frame_mesh, in_specs=in_specs, out_specs=out_specs, check_vma=False)
```

```python
import jax
import jax.numpy as jnp
from jax import lax
from jax.sharding import Mesh, PartitionSpec as P

W = 64


offsets = ((-1, -1), (-1, 0), (-1, 1), (0, -1), (0, 0), (0, 1), (1, -1), (1, 0), (1, 1))


def passed_along(value, axis, steps):
    count = lax.axis_size(axis)
    first, last = (max(0, -steps), min(count, count - steps))
    return lax.ppermute(value, axis, [(source, source + steps) for source in range(first, last)])


def scan_chunks(factor, value, reverse):
    count = value.shape[0]
    distance = 1
    while distance < count:
        if reverse:
            pads = ((0, distance), (0, 0), (0, 0))
            earlier_value = jnp.pad(value[distance:], pads)
            earlier_factor = jnp.pad(factor[distance:], pads)
        else:
            pads = ((distance, 0), (0, 0), (0, 0))
            earlier_value = jnp.pad(value[:-distance], pads)
            earlier_factor = jnp.pad(factor[:-distance], pads)
        value = value + factor * earlier_value
        factor = factor * earlier_factor
        distance *= 2
    return value


def pack_chunks(factor, value, count):
    rows, cells = value.shape
    chunk = rows // count
    factor_row = jnp.pad(factor.reshape(count, chunk), ((0, 0), (0, cells - chunk)))[:, None, :]
    return jnp.concatenate([value.reshape(count, chunk, cells), factor_row], axis=1)


def scan_owned(gathered, reverse):
    chunk = gathered.shape[1] - 1
    total = scan_chunks(gathered[:, chunk, :chunk][:, :, None], gathered[:, :chunk], reverse)
    if reverse:
        return jnp.pad(total[1:], ((0, 1), (0, 0), (0, 0)))
    return jnp.pad(total[:-1], ((1, 0), (0, 0), (0, 0)))


def shift_cells(source, row_shift, col_shift, grid_width):
    cell_count = source.shape[-1]
    margin = grid_width + 1
    padded = jnp.pad(source, [(0, 0)] * (source.ndim - 1) + [(margin, margin)])
    first_cell = margin + row_shift * grid_width + col_shift
    shifted = lax.slice_in_dim(padded, first_cell, first_cell + cell_count, axis=source.ndim - 1)
    column = jnp.arange(cell_count) % grid_width
    inside = (column + col_shift >= 0) & (column + col_shift < grid_width)
    return jnp.where(inside, shifted, jnp.zeros((), source.dtype))


def stencil_stack(source, grid_width, decay_factor):
    parts = [
        shift_cells(source, decay_factor * pair[0], decay_factor * pair[1], grid_width)
        for pair in offsets
    ]
    return jnp.stack(parts, axis=source.ndim - 2)


def stencil_conv(inputs, kernel, width):
    frames, chans, cells = inputs.shape
    image = inputs.reshape(frames, chans, cells // width, width)
    taps = kernel.reshape(3, 3, kernel.shape[1], chans).transpose(2, 3, 0, 1)
    out = lax.conv_general_dilated(
        image, taps, (1, 1), ((1, 1), (1, 1)), dimension_numbers=("NCHW", "OIHW", "NCHW"),
        preferred_element_type=jnp.float32,
    )
    return out.reshape(frames, kernel.shape[1], cells)


FRAME_AXES = ("chip", "core")


def pair_then_chip_sum(first, second):
    core = lax.axis_index("core")
    swap = [(0, 1), (1, 0)]
    first_flat, second_flat = first.reshape(-1), second.reshape(-1)
    kept = jnp.where(core == 0, first_flat, second_flat)
    sent = jnp.where(core == 0, second_flat, first_flat)
    pair_sum = (kept + lax.ppermute(sent, "core", swap)).reshape(lax.axis_size("chip"), -1)
    pieces = lax.all_to_all(pair_sum, "chip", 0, 0, tiled=True)
    reduced = jnp.sum(pieces, axis=0, keepdims=True)
    total = lax.all_to_all(jnp.broadcast_to(reduced, pieces.shape), "chip", 0, 0, tiled=True).reshape(-1)
    partner = lax.ppermute(total, "core", swap)
    first_total = jnp.where(core == 0, total, partner)
    second_total = jnp.where(core == 0, partner, total)
    return first_total.reshape(first.shape), second_total.reshape(second.shape)


def body(inputs, decay, kernel_b, kernel_c, cotangent):
    local_rows = kernel_b.shape[1]
    cell_count = inputs.shape[-1]
    blank_state = jnp.zeros((local_rows, cell_count), jnp.float32)
    drives = stencil_conv(inputs, kernel_b, W)

    def advance(current, frame_pair):
        frame_rate, drive = frame_pair
        current = frame_rate[:, None] * current + drive
        return (current, current)

    local_end, local_states = lax.scan(advance, blank_state, (decay, drives), unroll=True)
    decay_total = jnp.prod(decay, axis=0)
    blocks = lax.axis_size(FRAME_AXES)
    rows = local_end.shape[0]
    chunk = rows // blocks
    entering_owned = scan_owned(lax.all_to_all(pack_chunks(decay_total, local_end, blocks), FRAME_AXES, 0, 0, tiled=True), False)
    cot_stack = stencil_stack(cotangent, W, -1)
    injected = lax.psum_scatter(
        stencil_conv(cotangent, jnp.flip(kernel_c, 0).transpose(0, 2, 1), W),
        "chan",
        scatter_dimension=1,
        tiled=True,
    )
    entering_owned, injected = lax.optimization_barrier((entering_owned, injected))

    def retreat(carried, frame_pair):
        frame_rate, source = frame_pair
        adjoint = source + carried
        return (frame_rate[:, None] * adjoint, adjoint)

    message, local_adjoint = lax.scan(retreat, blank_state, (decay, injected), reverse=True, unroll=True)

    exchanged = lax.all_to_all(
        jnp.concatenate([entering_owned, pack_chunks(decay_total, message, blocks)], axis=1), FRAME_AXES, 0, 0, tiled=True
    )
    entering = exchanged[:, :chunk].reshape(rows, cell_count)
    arriving_owned = scan_owned(exchanged[:, chunk:], True)
    arriving = lax.all_to_all(arriving_owned, FRAME_AXES, 0, 0, tiled=True).reshape(rows, cell_count)
    cumulative = jnp.cumprod(decay, axis=0)
    states = local_states + cumulative[:, :, None] * entering[None]
    previous = jnp.concatenate([entering[None], states[:-1]], axis=0)
    states_bf = states.astype(jnp.bfloat16)
    suffix = jnp.flip(jnp.cumprod(jnp.flip(decay, 0), 0), 0)
    later_decay = jnp.concatenate([suffix[1:], jnp.ones_like(decay[:1])], axis=0)
    adjoint = local_adjoint + later_decay[:, :, None] * arriving[None]
    decay_grad = jnp.sum(adjoint * previous, axis=2)
    adjoint_bf = adjoint.astype(jnp.bfloat16)
    input_stack = stencil_stack(inputs, W, 1)
    grad_b_part = jnp.einsum(
        "fps,fkcs->kpc", adjoint_bf, input_stack, preferred_element_type=jnp.float32
    )
    all_states = lax.all_gather(states_bf, "chan", axis=1, tiled=True)
    grad_c_part = jnp.einsum(
        "fkus,fps->kup", cot_stack, all_states, preferred_element_type=jnp.float32
    )
    grad_b, grad_c = pair_then_chip_sum(grad_b_part, grad_c_part)
    return (grad_b, grad_c, decay_grad)


def solution(mesh):
    chan = mesh.shape["chan"]
    frame_mesh = Mesh(mesh.devices.reshape(-1, 2, chan), (*FRAME_AXES, "chan"))
    in_specs = (
        P(FRAME_AXES, None, None),
        P(FRAME_AXES, "chan"),
        P(None, "chan", None),
        P(None, "chan", None),
        P(FRAME_AXES, "chan", None),
    )
    out_specs = (P(None, "chan", None), P(None, "chan", None), P(FRAME_AXES, "chan"))
    return jax.shard_map(body, mesh=frame_mesh, in_specs=in_specs, out_specs=out_specs, check_vma=False)
```

```python
import jax
import jax.numpy as jnp
from jax import lax
from jax.sharding import Mesh, PartitionSpec as P

W = 64


offsets = ((-1, -1), (-1, 0), (-1, 1), (0, -1), (0, 0), (0, 1), (1, -1), (1, 0), (1, 1))


def passed_along(value, axis, steps):
    count = lax.axis_size(axis)
    first, last = (max(0, -steps), min(count, count - steps))
    return lax.ppermute(value, axis, [(source, source + steps) for source in range(first, last)])


def scan_chunks(factor, value, reverse):
    count = value.shape[0]
    distance = 1
    while distance < count:
        if reverse:
            pads = ((0, distance), (0, 0), (0, 0))
            earlier_value = jnp.pad(value[distance:], pads)
            earlier_factor = jnp.pad(factor[distance:], pads)
        else:
            pads = ((distance, 0), (0, 0), (0, 0))
            earlier_value = jnp.pad(value[:-distance], pads)
            earlier_factor = jnp.pad(factor[:-distance], pads)
        value = value + factor * earlier_value
        factor = factor * earlier_factor
        distance *= 2
    return value


def pack_chunks(factor, value, count):
    rows, cells = value.shape
    chunk = rows // count
    factor_row = jnp.pad(factor.reshape(count, chunk), ((0, 0), (0, cells - chunk)))[:, None, :]
    return jnp.concatenate([value.reshape(count, chunk, cells), factor_row], axis=1)


def scan_owned(gathered, reverse):
    chunk = gathered.shape[1] - 1
    total = scan_chunks(gathered[:, chunk, :chunk][:, :, None], gathered[:, :chunk], reverse)
    if reverse:
        return jnp.pad(total[1:], ((0, 1), (0, 0), (0, 0)))
    return jnp.pad(total[:-1], ((1, 0), (0, 0), (0, 0)))


def shift_cells(source, row_shift, col_shift, grid_width):
    cell_count = source.shape[-1]
    margin = grid_width + 1
    padded = jnp.pad(source, [(0, 0)] * (source.ndim - 1) + [(margin, margin)])
    first_cell = margin + row_shift * grid_width + col_shift
    shifted = lax.slice_in_dim(padded, first_cell, first_cell + cell_count, axis=source.ndim - 1)
    column = jnp.arange(cell_count) % grid_width
    inside = (column + col_shift >= 0) & (column + col_shift < grid_width)
    return jnp.where(inside, shifted, jnp.zeros((), source.dtype))


def stencil_stack(source, grid_width, decay_factor):
    parts = [
        shift_cells(source, decay_factor * pair[0], decay_factor * pair[1], grid_width)
        for pair in offsets
    ]
    return jnp.stack(parts, axis=source.ndim - 2)


def stencil_conv(inputs, kernel, width):
    frames, chans, cells = inputs.shape
    image = inputs.reshape(frames, chans, cells // width, width)
    taps = kernel.reshape(3, 3, kernel.shape[1], chans).transpose(2, 3, 0, 1)
    out = lax.conv_general_dilated(
        image, taps, (1, 1), ((1, 1), (1, 1)), dimension_numbers=("NCHW", "OIHW", "NCHW"),
        preferred_element_type=jnp.float32,
    )
    return out.reshape(frames, kernel.shape[1], cells)


FRAME_AXES = ("chip", "core")


def pair_then_chip_sum(first, second):
    core = lax.axis_index("core")
    swap = [(0, 1), (1, 0)]
    first_flat, second_flat = first.reshape(-1), second.reshape(-1)
    kept = jnp.where(core == 0, first_flat, second_flat)
    sent = jnp.where(core == 0, second_flat, first_flat)
    pair_sum = (kept + lax.ppermute(sent, "core", swap)).reshape(lax.axis_size("chip"), -1)
    pieces = lax.all_to_all(pair_sum, "chip", 0, 0, tiled=True)
    reduced = jnp.sum(pieces, axis=0, keepdims=True)
    total = lax.all_to_all(jnp.broadcast_to(reduced, pieces.shape), "chip", 0, 0, tiled=True).reshape(-1)
    partner = lax.ppermute(total, "core", swap)
    first_total = jnp.where(core == 0, total, partner)
    second_total = jnp.where(core == 0, partner, total)
    return first_total.reshape(first.shape), second_total.reshape(second.shape)


def body(inputs, decay, kernel_b, kernel_c, cotangent):
    local_rows = kernel_b.shape[1]
    cell_count = inputs.shape[-1]
    blank_state = jnp.zeros((local_rows, cell_count), jnp.float32)
    drives = stencil_conv(inputs, kernel_b, W)

    def advance(current, frame_pair):
        frame_rate, drive = frame_pair
        current = frame_rate[:, None] * current + drive
        return (current, current)

    local_end, local_states = lax.scan(advance, blank_state, (decay, drives), unroll=True)
    decay_total = jnp.prod(decay, axis=0)
    blocks = lax.axis_size(FRAME_AXES)
    rows = local_end.shape[0]
    chunk = rows // blocks
    entering_owned = scan_owned(lax.all_to_all(pack_chunks(decay_total, local_end, blocks), FRAME_AXES, 0, 0, tiled=True), False)
    cot_stack = stencil_stack(cotangent, W, -1)
    injected = lax.psum_scatter(
        jnp.einsum("kup,fkus->pfs", kernel_c, cot_stack, preferred_element_type=jnp.float32),
        "chan",
        scatter_dimension=0,
        tiled=True,
    )
    entering_owned, injected = lax.optimization_barrier((entering_owned, injected))
    injected = jnp.moveaxis(injected, 1, 0)

    def retreat(carried, frame_pair):
        frame_rate, source = frame_pair
        adjoint = source + carried
        return (frame_rate[:, None] * adjoint, adjoint)

    message, local_adjoint = lax.scan(retreat, blank_state, (decay, injected), reverse=True, unroll=True)

    exchanged = lax.all_to_all(
        jnp.concatenate([entering_owned, pack_chunks(decay_total, message, blocks)], axis=1), FRAME_AXES, 0, 0, tiled=True
    )
    entering = exchanged[:, :chunk].reshape(rows, cell_count)
    arriving_owned = scan_owned(exchanged[:, chunk:], True)
    arriving = lax.all_to_all(arriving_owned, FRAME_AXES, 0, 0, tiled=True).reshape(rows, cell_count)
    cumulative = jnp.cumprod(decay, axis=0)
    states = local_states + cumulative[:, :, None] * entering[None]
    previous = jnp.concatenate([entering[None], states[:-1]], axis=0)
    states_bf = states.astype(jnp.bfloat16)
    suffix = jnp.flip(jnp.cumprod(jnp.flip(decay, 0), 0), 0)
    later_decay = jnp.concatenate([suffix[1:], jnp.ones_like(decay[:1])], axis=0)
    adjoint = local_adjoint + later_decay[:, :, None] * arriving[None]
    decay_grad = jnp.sum(adjoint * previous, axis=2)
    adjoint_bf = adjoint.astype(jnp.bfloat16)
    input_stack = stencil_stack(inputs, W, 1)
    grad_b_part = jnp.einsum(
        "fps,fkcs->kpc", adjoint_bf, input_stack, preferred_element_type=jnp.float32
    )
    all_states = lax.all_gather(states_bf, "chan", axis=1, tiled=True)
    grad_c_part = jnp.einsum(
        "fkus,fps->kup", cot_stack, all_states, preferred_element_type=jnp.float32
    )
    grad_b, grad_c = pair_then_chip_sum(grad_b_part, grad_c_part)
    return (grad_b, grad_c, decay_grad)


def solution(mesh):
    chan = mesh.shape["chan"]
    frame_mesh = Mesh(mesh.devices.reshape(-1, 2, chan), (*FRAME_AXES, "chan"))
    in_specs = (
        P(FRAME_AXES, None, None),
        P(FRAME_AXES, "chan"),
        P(None, "chan", None),
        P(None, "chan", None),
        P(FRAME_AXES, "chan", None),
    )
    out_specs = (P(None, "chan", None), P(None, "chan", None), P(FRAME_AXES, "chan"))
    return jax.shard_map(body, mesh=frame_mesh, in_specs=in_specs, out_specs=out_specs, check_vma=False)
```

```python
import jax
import jax.numpy as jnp
from jax import lax
from jax.sharding import Mesh, PartitionSpec as P

W = 64


offsets = ((-1, -1), (-1, 0), (-1, 1), (0, -1), (0, 0), (0, 1), (1, -1), (1, 0), (1, 1))


def passed_along(value, axis, steps):
    count = lax.axis_size(axis)
    first, last = (max(0, -steps), min(count, count - steps))
    return lax.ppermute(value, axis, [(source, source + steps) for source in range(first, last)])


def scan_chunks(factor, value, reverse):
    count = value.shape[0]
    distance = 1
    while distance < count:
        if reverse:
            pads = ((0, distance), (0, 0), (0, 0))
            earlier_value = jnp.pad(value[distance:], pads)
            earlier_factor = jnp.pad(factor[distance:], pads)
        else:
            pads = ((distance, 0), (0, 0), (0, 0))
            earlier_value = jnp.pad(value[:-distance], pads)
            earlier_factor = jnp.pad(factor[:-distance], pads)
        value = value + factor * earlier_value
        factor = factor * earlier_factor
        distance *= 2
    return value


def pack_chunks(factor, value, count):
    rows, cells = value.shape
    chunk = rows // count
    factor_row = jnp.pad(factor.reshape(count, chunk), ((0, 0), (0, cells - chunk)))[:, None, :]
    return jnp.concatenate([value.reshape(count, chunk, cells), factor_row], axis=1)


def scan_owned(gathered, reverse):
    chunk = gathered.shape[1] - 1
    total = scan_chunks(gathered[:, chunk, :chunk][:, :, None], gathered[:, :chunk], reverse)
    if reverse:
        return jnp.pad(total[1:], ((0, 1), (0, 0), (0, 0)))
    return jnp.pad(total[:-1], ((1, 0), (0, 0), (0, 0)))


def shift_cells(source, row_shift, col_shift, grid_width):
    cell_count = source.shape[-1]
    margin = grid_width + 1
    padded = jnp.pad(source, [(0, 0)] * (source.ndim - 1) + [(margin, margin)])
    first_cell = margin + row_shift * grid_width + col_shift
    shifted = lax.slice_in_dim(padded, first_cell, first_cell + cell_count, axis=source.ndim - 1)
    column = jnp.arange(cell_count) % grid_width
    inside = (column + col_shift >= 0) & (column + col_shift < grid_width)
    return jnp.where(inside, shifted, jnp.zeros((), source.dtype))


def stencil_stack(source, grid_width, decay_factor):
    parts = [
        shift_cells(source, decay_factor * pair[0], decay_factor * pair[1], grid_width)
        for pair in offsets
    ]
    return jnp.stack(parts, axis=source.ndim - 2)


def stencil_conv(inputs, kernel, width):
    frames, chans, cells = inputs.shape
    image = inputs.reshape(frames, chans, cells // width, width)
    taps = kernel.reshape(3, 3, kernel.shape[1], chans).transpose(2, 3, 0, 1)
    out = lax.conv_general_dilated(
        image, taps, (1, 1), ((1, 1), (1, 1)), dimension_numbers=("NCHW", "OIHW", "NCHW"),
        preferred_element_type=jnp.float32,
    )
    return out.reshape(frames, kernel.shape[1], cells)


def gather_readout(cotangent, kernel_c, states_local, axis):
    count = lax.axis_size(axis)
    me = lax.axis_index(axis)
    cot_blocks = [cotangent]
    kernel_blocks = [lax.dynamic_slice_in_dim(kernel_c, me * states_local, states_local, axis=2)]
    for step in range(1, count):
        pairs = [(source, (source + step) % count) for source in range(count)]
        wanted = lax.dynamic_slice_in_dim(kernel_c, ((me + step) % count) * states_local, states_local, axis=2)
        cot_blocks.append(lax.ppermute(cotangent, axis, pairs))
        kernel_blocks.append(lax.ppermute(wanted, axis, pairs))
    return jnp.concatenate(cot_blocks, axis=1), jnp.concatenate(kernel_blocks, axis=1)


FRAME_AXES = ("chip", "core")


def pair_then_chip_sum(first, second):
    core = lax.axis_index("core")
    swap = [(0, 1), (1, 0)]
    first_flat, second_flat = first.reshape(-1), second.reshape(-1)
    kept = jnp.where(core == 0, first_flat, second_flat)
    sent = jnp.where(core == 0, second_flat, first_flat)
    pair_sum = (kept + lax.ppermute(sent, "core", swap)).reshape(lax.axis_size("chip"), -1)
    pieces = lax.all_to_all(pair_sum, "chip", 0, 0, tiled=True)
    reduced = jnp.sum(pieces, axis=0, keepdims=True)
    total = lax.all_to_all(jnp.broadcast_to(reduced, pieces.shape), "chip", 0, 0, tiled=True).reshape(-1)
    partner = lax.ppermute(total, "core", swap)
    first_total = jnp.where(core == 0, total, partner)
    second_total = jnp.where(core == 0, partner, total)
    return first_total.reshape(first.shape), second_total.reshape(second.shape)


def body(inputs, decay, kernel_b, kernel_c, cotangent):
    local_rows = kernel_b.shape[1]
    cell_count = inputs.shape[-1]
    blank_state = jnp.zeros((local_rows, cell_count), jnp.float32)
    drives = stencil_conv(inputs, kernel_b, W)

    def advance(current, frame_pair):
        frame_rate, drive = frame_pair
        current = frame_rate[:, None] * current + drive
        return (current, current)

    local_end, local_states = lax.scan(advance, blank_state, (decay, drives))
    decay_total = jnp.prod(decay, axis=0)
    blocks = lax.axis_size(FRAME_AXES)
    rows = local_end.shape[0]
    chunk = rows // blocks
    entering_owned = scan_owned(lax.all_to_all(pack_chunks(decay_total, local_end, blocks), FRAME_AXES, 0, 0, tiled=True), False)
    cot_stack = stencil_stack(cotangent, W, -1)
    all_cotangent, readout_local = gather_readout(cotangent, kernel_c, kernel_b.shape[1], "chan")
    injected = stencil_conv(all_cotangent, jnp.flip(readout_local, 0).transpose(0, 2, 1), W)
    entering_owned, injected = lax.optimization_barrier((entering_owned, injected))

    def retreat(carried, frame_pair):
        frame_rate, source = frame_pair
        adjoint = source + carried
        return (frame_rate[:, None] * adjoint, adjoint)

    message, local_adjoint = lax.scan(retreat, blank_state, (decay, injected), reverse=True)

    exchanged = lax.all_to_all(
        jnp.concatenate([entering_owned, pack_chunks(decay_total, message, blocks)], axis=1), FRAME_AXES, 0, 0, tiled=True
    )
    entering = exchanged[:, :chunk].reshape(rows, cell_count)
    arriving_owned = scan_owned(exchanged[:, chunk:], True)
    arriving = lax.all_to_all(arriving_owned, FRAME_AXES, 0, 0, tiled=True).reshape(rows, cell_count)
    cumulative = jnp.cumprod(decay, axis=0)
    states = local_states + cumulative[:, :, None] * entering[None]
    previous = jnp.concatenate([entering[None], states[:-1]], axis=0)
    states_bf = states.astype(jnp.bfloat16)
    suffix = jnp.flip(jnp.cumprod(jnp.flip(decay, 0), 0), 0)
    later_decay = jnp.concatenate([suffix[1:], jnp.ones_like(decay[:1])], axis=0)
    adjoint = local_adjoint + later_decay[:, :, None] * arriving[None]
    decay_grad = jnp.sum(adjoint * previous, axis=2)
    adjoint_bf = adjoint.astype(jnp.bfloat16)
    input_stack = stencil_stack(inputs, W, 1)
    grad_b_part = jnp.einsum(
        "fps,fkcs->kpc", adjoint_bf, input_stack, preferred_element_type=jnp.float32
    )
    all_states = lax.all_gather(states_bf, "chan", axis=1, tiled=True)
    grad_c_part = jnp.einsum(
        "fkus,fps->kup", cot_stack, all_states, preferred_element_type=jnp.float32
    )
    grad_b, grad_c = pair_then_chip_sum(grad_b_part, grad_c_part)
    return (grad_b, grad_c, decay_grad)


def solution(mesh):
    chan = mesh.shape["chan"]
    frame_mesh = Mesh(mesh.devices.reshape(-1, 2, chan), (*FRAME_AXES, "chan"))
    in_specs = (
        P(FRAME_AXES, None, None),
        P(FRAME_AXES, "chan"),
        P(None, "chan", None),
        P(None, "chan", None),
        P(FRAME_AXES, "chan", None),
    )
    out_specs = (P(None, "chan", None), P(None, "chan", None), P(FRAME_AXES, "chan"))
    return jax.shard_map(body, mesh=frame_mesh, in_specs=in_specs, out_specs=out_specs, check_vma=False)
```

```python
import jax
import jax.numpy as jnp
from jax import lax
from jax.sharding import Mesh, PartitionSpec as P

W = 64


offsets = ((-1, -1), (-1, 0), (-1, 1), (0, -1), (0, 0), (0, 1), (1, -1), (1, 0), (1, 1))


def passed_along(value, axis, steps):
    count = lax.axis_size(axis)
    first, last = (max(0, -steps), min(count, count - steps))
    return lax.ppermute(value, axis, [(source, source + steps) for source in range(first, last)])


def scan_chunks(factor, value, reverse):
    count = value.shape[0]
    distance = 1
    while distance < count:
        if reverse:
            pads = ((0, distance), (0, 0), (0, 0))
            earlier_value = jnp.pad(value[distance:], pads)
            earlier_factor = jnp.pad(factor[distance:], pads)
        else:
            pads = ((distance, 0), (0, 0), (0, 0))
            earlier_value = jnp.pad(value[:-distance], pads)
            earlier_factor = jnp.pad(factor[:-distance], pads)
        value = value + factor * earlier_value
        factor = factor * earlier_factor
        distance *= 2
    return value


def pack_chunks(factor, value, count):
    rows, cells = value.shape
    chunk = rows // count
    factor_row = jnp.pad(factor.reshape(count, chunk), ((0, 0), (0, cells - chunk)))[:, None, :]
    return jnp.concatenate([value.reshape(count, chunk, cells), factor_row], axis=1)


def scan_owned(gathered, reverse):
    chunk = gathered.shape[1] - 1
    total = scan_chunks(gathered[:, chunk, :chunk][:, :, None], gathered[:, :chunk], reverse)
    if reverse:
        return jnp.pad(total[1:], ((0, 1), (0, 0), (0, 0)))
    return jnp.pad(total[:-1], ((1, 0), (0, 0), (0, 0)))


def shift_cells(source, row_shift, col_shift, grid_width):
    cell_count = source.shape[-1]
    margin = grid_width + 1
    padded = jnp.pad(source, [(0, 0)] * (source.ndim - 1) + [(margin, margin)])
    first_cell = margin + row_shift * grid_width + col_shift
    shifted = lax.slice_in_dim(padded, first_cell, first_cell + cell_count, axis=source.ndim - 1)
    column = jnp.arange(cell_count) % grid_width
    inside = (column + col_shift >= 0) & (column + col_shift < grid_width)
    return jnp.where(inside, shifted, jnp.zeros((), source.dtype))


def stencil_stack(source, grid_width, decay_factor):
    parts = [
        shift_cells(source, decay_factor * pair[0], decay_factor * pair[1], grid_width)
        for pair in offsets
    ]
    return jnp.stack(parts, axis=source.ndim - 2)


def stencil_conv(inputs, kernel, width):
    frames, chans, cells = inputs.shape
    image = inputs.reshape(frames, chans, cells // width, width)
    taps = kernel.reshape(3, 3, kernel.shape[1], chans).transpose(2, 3, 0, 1)
    out = lax.conv_general_dilated(
        image, taps, (1, 1), ((1, 1), (1, 1)), dimension_numbers=("NCHW", "OIHW", "NCHW"),
        preferred_element_type=jnp.float32,
    )
    return out.reshape(frames, kernel.shape[1], cells)


def gather_readout(cotangent, kernel_c, states_local, axis):
    count = lax.axis_size(axis)
    me = lax.axis_index(axis)
    cot_blocks = [cotangent]
    kernel_blocks = [lax.dynamic_slice_in_dim(kernel_c, me * states_local, states_local, axis=2)]
    for step in range(1, count):
        pairs = [(source, (source + step) % count) for source in range(count)]
        wanted = lax.dynamic_slice_in_dim(kernel_c, ((me + step) % count) * states_local, states_local, axis=2)
        packed = lax.ppermute(jnp.concatenate([cotangent.reshape(-1), wanted.reshape(-1)]), axis, pairs)
        cot_blocks.append(packed[: cotangent.size].reshape(cotangent.shape))
        kernel_blocks.append(packed[cotangent.size :].reshape(wanted.shape))
    return jnp.concatenate(cot_blocks, axis=1), jnp.concatenate(kernel_blocks, axis=1)


FRAME_AXES = ("chip", "core")


def pair_then_chip_sum(first, second):
    core = lax.axis_index("core")
    swap = [(0, 1), (1, 0)]
    first_flat, second_flat = first.reshape(-1), second.reshape(-1)
    kept = jnp.where(core == 0, first_flat, second_flat)
    sent = jnp.where(core == 0, second_flat, first_flat)
    pair_sum = (kept + lax.ppermute(sent, "core", swap)).reshape(lax.axis_size("chip"), -1)
    pieces = lax.all_to_all(pair_sum, "chip", 0, 0, tiled=True)
    reduced = jnp.sum(pieces, axis=0, keepdims=True)
    total = lax.all_to_all(jnp.broadcast_to(reduced, pieces.shape), "chip", 0, 0, tiled=True).reshape(-1)
    partner = lax.ppermute(total, "core", swap)
    first_total = jnp.where(core == 0, total, partner)
    second_total = jnp.where(core == 0, partner, total)
    return first_total.reshape(first.shape), second_total.reshape(second.shape)


def body(inputs, decay, kernel_b, kernel_c, cotangent):
    local_rows = kernel_b.shape[1]
    cell_count = inputs.shape[-1]
    blank_state = jnp.zeros((local_rows, cell_count), jnp.float32)
    drives = stencil_conv(inputs, kernel_b, W)

    def advance(current, frame_pair):
        frame_rate, drive = frame_pair
        current = frame_rate[:, None] * current + drive
        return (current, current)

    local_end, local_states = lax.scan(advance, blank_state, (decay, drives))
    decay_total = jnp.prod(decay, axis=0)
    blocks = lax.axis_size(FRAME_AXES)
    rows = local_end.shape[0]
    chunk = rows // blocks
    entering_owned = scan_owned(lax.all_to_all(pack_chunks(decay_total, local_end, blocks), FRAME_AXES, 0, 0, tiled=True), False)
    cot_stack = stencil_stack(cotangent, W, -1)
    all_cotangent, readout_local = gather_readout(cotangent, kernel_c, kernel_b.shape[1], "chan")
    injected = stencil_conv(all_cotangent, jnp.flip(readout_local, 0).transpose(0, 2, 1), W)
    entering_owned, injected = lax.optimization_barrier((entering_owned, injected))

    def retreat(carried, frame_pair):
        frame_rate, source = frame_pair
        adjoint = source + carried
        return (frame_rate[:, None] * adjoint, adjoint)

    message, local_adjoint = lax.scan(retreat, blank_state, (decay, injected), reverse=True)

    exchanged = lax.all_to_all(
        jnp.concatenate([entering_owned, pack_chunks(decay_total, message, blocks)], axis=1), FRAME_AXES, 0, 0, tiled=True
    )
    entering = exchanged[:, :chunk].reshape(rows, cell_count)
    arriving_owned = scan_owned(exchanged[:, chunk:], True)
    arriving = lax.all_to_all(arriving_owned, FRAME_AXES, 0, 0, tiled=True).reshape(rows, cell_count)
    cumulative = jnp.cumprod(decay, axis=0)
    states = local_states + cumulative[:, :, None] * entering[None]
    previous = jnp.concatenate([entering[None], states[:-1]], axis=0)
    states_bf = states.astype(jnp.bfloat16)
    suffix = jnp.flip(jnp.cumprod(jnp.flip(decay, 0), 0), 0)
    later_decay = jnp.concatenate([suffix[1:], jnp.ones_like(decay[:1])], axis=0)
    adjoint = local_adjoint + later_decay[:, :, None] * arriving[None]
    decay_grad = jnp.sum(adjoint * previous, axis=2)
    adjoint_bf = adjoint.astype(jnp.bfloat16)
    input_stack = stencil_stack(inputs, W, 1)
    grad_b_part = jnp.einsum(
        "fps,fkcs->kpc", adjoint_bf, input_stack, preferred_element_type=jnp.float32
    )
    all_states = lax.all_gather(states_bf, "chan", axis=1, tiled=True)
    grad_c_part = jnp.einsum(
        "fkus,fps->kup", cot_stack, all_states, preferred_element_type=jnp.float32
    )
    grad_b, grad_c = pair_then_chip_sum(grad_b_part, grad_c_part)
    return (grad_b, grad_c, decay_grad)


def solution(mesh):
    chan = mesh.shape["chan"]
    frame_mesh = Mesh(mesh.devices.reshape(-1, 2, chan), (*FRAME_AXES, "chan"))
    in_specs = (
        P(FRAME_AXES, None, None),
        P(FRAME_AXES, "chan"),
        P(None, "chan", None),
        P(None, "chan", None),
        P(FRAME_AXES, "chan", None),
    )
    out_specs = (P(None, "chan", None), P(None, "chan", None), P(FRAME_AXES, "chan"))
    return jax.shard_map(body, mesh=frame_mesh, in_specs=in_specs, out_specs=out_specs, check_vma=False)
```

```python
import jax
import jax.numpy as jnp
from jax import lax
from jax.sharding import Mesh, PartitionSpec as P

W = 64


offsets = ((-1, -1), (-1, 0), (-1, 1), (0, -1), (0, 0), (0, 1), (1, -1), (1, 0), (1, 1))


def passed_along(value, axis, steps):
    count = lax.axis_size(axis)
    first, last = (max(0, -steps), min(count, count - steps))
    return lax.ppermute(value, axis, [(source, source + steps) for source in range(first, last)])


def scan_chunks(factor, value, reverse):
    count = value.shape[0]
    distance = 1
    while distance < count:
        if reverse:
            pads = ((0, distance), (0, 0), (0, 0))
            earlier_value = jnp.pad(value[distance:], pads)
            earlier_factor = jnp.pad(factor[distance:], pads)
        else:
            pads = ((distance, 0), (0, 0), (0, 0))
            earlier_value = jnp.pad(value[:-distance], pads)
            earlier_factor = jnp.pad(factor[:-distance], pads)
        value = value + factor * earlier_value
        factor = factor * earlier_factor
        distance *= 2
    return value


def pack_chunks(factor, value, count):
    rows, cells = value.shape
    chunk = rows // count
    factor_row = jnp.pad(factor.reshape(count, chunk), ((0, 0), (0, cells - chunk)))[:, None, :]
    return jnp.concatenate([value.reshape(count, chunk, cells), factor_row], axis=1)


def scan_owned(gathered, reverse):
    chunk = gathered.shape[1] - 1
    total = scan_chunks(gathered[:, chunk, :chunk][:, :, None], gathered[:, :chunk], reverse)
    if reverse:
        return jnp.pad(total[1:], ((0, 1), (0, 0), (0, 0)))
    return jnp.pad(total[:-1], ((1, 0), (0, 0), (0, 0)))


def shift_cells(source, row_shift, col_shift, grid_width):
    cell_count = source.shape[-1]
    margin = grid_width + 1
    padded = jnp.pad(source, [(0, 0)] * (source.ndim - 1) + [(margin, margin)])
    first_cell = margin + row_shift * grid_width + col_shift
    shifted = lax.slice_in_dim(padded, first_cell, first_cell + cell_count, axis=source.ndim - 1)
    column = jnp.arange(cell_count) % grid_width
    inside = (column + col_shift >= 0) & (column + col_shift < grid_width)
    return jnp.where(inside, shifted, jnp.zeros((), source.dtype))


def stencil_stack(source, grid_width, decay_factor):
    parts = [
        shift_cells(source, decay_factor * pair[0], decay_factor * pair[1], grid_width)
        for pair in offsets
    ]
    return jnp.stack(parts, axis=source.ndim - 2)


def stencil_conv(inputs, kernel, width):
    frames, chans, cells = inputs.shape
    image = inputs.reshape(frames, chans, cells // width, width)
    taps = kernel.reshape(3, 3, kernel.shape[1], chans).transpose(2, 3, 0, 1)
    out = lax.conv_general_dilated(
        image, taps, (1, 1), ((1, 1), (1, 1)), dimension_numbers=("NCHW", "OIHW", "NCHW"),
        preferred_element_type=jnp.float32,
    )
    return out.reshape(frames, kernel.shape[1], cells)


def gather_readout(cotangent, kernel_c, states_local, axis):
    count = lax.axis_size(axis)
    me = lax.axis_index(axis)
    cot_blocks = [cotangent]
    kernel_blocks = [lax.dynamic_slice_in_dim(kernel_c, me * states_local, states_local, axis=2)]
    for step in range(1, count):
        pairs = [(source, (source + step) % count) for source in range(count)]
        wanted = lax.dynamic_slice_in_dim(kernel_c, ((me + step) % count) * states_local, states_local, axis=2)
        cot_blocks.append(lax.ppermute(cotangent, axis, pairs))
        kernel_blocks.append(lax.ppermute(wanted, axis, pairs))
    return jnp.concatenate(cot_blocks, axis=1), jnp.concatenate(kernel_blocks, axis=1)


FRAME_AXES = ("chip", "core")


def pair_then_chip_sum(first, second):
    core = lax.axis_index("core")
    swap = [(0, 1), (1, 0)]
    first_flat, second_flat = first.reshape(-1), second.reshape(-1)
    kept = jnp.where(core == 0, first_flat, second_flat)
    sent = jnp.where(core == 0, second_flat, first_flat)
    pair_sum = (kept + lax.ppermute(sent, "core", swap)).reshape(lax.axis_size("chip"), -1)
    pieces = lax.all_to_all(pair_sum, "chip", 0, 0, tiled=True)
    reduced = jnp.sum(pieces, axis=0, keepdims=True)
    total = lax.all_to_all(jnp.broadcast_to(reduced, pieces.shape), "chip", 0, 0, tiled=True).reshape(-1)
    partner = lax.ppermute(total, "core", swap)
    first_total = jnp.where(core == 0, total, partner)
    second_total = jnp.where(core == 0, partner, total)
    return first_total.reshape(first.shape), second_total.reshape(second.shape)


def body(inputs, decay, kernel_b, kernel_c, cotangent):
    local_rows = kernel_b.shape[1]
    cell_count = inputs.shape[-1]
    blank_state = jnp.zeros((local_rows, cell_count), jnp.float32)
    drives = stencil_conv(inputs, kernel_b, W)

    def advance(current, frame_pair):
        frame_rate, drive = frame_pair
        current = frame_rate[:, None] * current + drive
        return (current, current)

    local_end, local_states = lax.scan(advance, blank_state, (decay, drives))
    decay_total = jnp.prod(decay, axis=0)
    blocks = lax.axis_size(FRAME_AXES)
    rows = local_end.shape[0]
    chunk = rows // blocks
    entering_owned = scan_owned(lax.all_to_all(pack_chunks(decay_total, local_end, blocks), FRAME_AXES, 0, 0, tiled=True), False)
    all_cotangent, readout_local = gather_readout(cotangent, kernel_c, kernel_b.shape[1], "chan")
    injected = stencil_conv(all_cotangent, jnp.flip(readout_local, 0).transpose(0, 2, 1), W)
    entering_owned, injected = lax.optimization_barrier((entering_owned, injected))

    def retreat(carried, frame_pair):
        frame_rate, source = frame_pair
        adjoint = source + carried
        return (frame_rate[:, None] * adjoint, adjoint)

    message, local_adjoint = lax.scan(retreat, blank_state, (decay, injected), reverse=True)

    exchanged = lax.all_to_all(
        jnp.concatenate([entering_owned, pack_chunks(decay_total, message, blocks)], axis=1), FRAME_AXES, 0, 0, tiled=True
    )
    entering = exchanged[:, :chunk].reshape(rows, cell_count)
    entering, late_cotangent = lax.optimization_barrier((entering, cotangent))
    cot_stack = stencil_stack(late_cotangent, W, -1)
    arriving_owned = scan_owned(exchanged[:, chunk:], True)
    arriving = lax.all_to_all(arriving_owned, FRAME_AXES, 0, 0, tiled=True).reshape(rows, cell_count)
    cumulative = jnp.cumprod(decay, axis=0)
    states = local_states + cumulative[:, :, None] * entering[None]
    previous = jnp.concatenate([entering[None], states[:-1]], axis=0)
    states_bf = states.astype(jnp.bfloat16)
    suffix = jnp.flip(jnp.cumprod(jnp.flip(decay, 0), 0), 0)
    later_decay = jnp.concatenate([suffix[1:], jnp.ones_like(decay[:1])], axis=0)
    adjoint = local_adjoint + later_decay[:, :, None] * arriving[None]
    decay_grad = jnp.sum(adjoint * previous, axis=2)
    adjoint_bf = adjoint.astype(jnp.bfloat16)
    input_stack = stencil_stack(inputs, W, 1)
    grad_b_part = jnp.einsum(
        "fps,fkcs->kpc", adjoint_bf, input_stack, preferred_element_type=jnp.float32
    )
    all_states = lax.all_gather(states_bf, "chan", axis=1, tiled=True)
    grad_c_part = jnp.einsum(
        "fkus,fps->kup", cot_stack, all_states, preferred_element_type=jnp.float32
    )
    grad_b, grad_c = pair_then_chip_sum(grad_b_part, grad_c_part)
    return (grad_b, grad_c, decay_grad)


def solution(mesh):
    chan = mesh.shape["chan"]
    frame_mesh = Mesh(mesh.devices.reshape(-1, 2, chan), (*FRAME_AXES, "chan"))
    in_specs = (
        P(FRAME_AXES, None, None),
        P(FRAME_AXES, "chan"),
        P(None, "chan", None),
        P(None, "chan", None),
        P(FRAME_AXES, "chan", None),
    )
    out_specs = (P(None, "chan", None), P(None, "chan", None), P(FRAME_AXES, "chan"))
    return jax.shard_map(body, mesh=frame_mesh, in_specs=in_specs, out_specs=out_specs, check_vma=False)
```

```python
import jax
import jax.numpy as jnp
from jax import lax
from jax.sharding import Mesh, PartitionSpec as P

W = 64


offsets = ((-1, -1), (-1, 0), (-1, 1), (0, -1), (0, 0), (0, 1), (1, -1), (1, 0), (1, 1))


def passed_along(value, axis, steps):
    count = lax.axis_size(axis)
    first, last = (max(0, -steps), min(count, count - steps))
    return lax.ppermute(value, axis, [(source, source + steps) for source in range(first, last)])


def scan_chunks(factor, value, reverse):
    count = value.shape[0]
    distance = 1
    while distance < count:
        if reverse:
            pads = ((0, distance), (0, 0), (0, 0))
            earlier_value = jnp.pad(value[distance:], pads)
            earlier_factor = jnp.pad(factor[distance:], pads)
        else:
            pads = ((distance, 0), (0, 0), (0, 0))
            earlier_value = jnp.pad(value[:-distance], pads)
            earlier_factor = jnp.pad(factor[:-distance], pads)
        value = value + factor * earlier_value
        factor = factor * earlier_factor
        distance *= 2
    return value


def pack_chunks(factor, value, count):
    rows, cells = value.shape
    chunk = rows // count
    factor_row = jnp.pad(factor.reshape(count, chunk), ((0, 0), (0, cells - chunk)))[:, None, :]
    return jnp.concatenate([value.reshape(count, chunk, cells), factor_row], axis=1)


def scan_owned(gathered, reverse):
    chunk = gathered.shape[1] - 1
    total = scan_chunks(gathered[:, chunk, :chunk][:, :, None], gathered[:, :chunk], reverse)
    if reverse:
        return jnp.pad(total[1:], ((0, 1), (0, 0), (0, 0)))
    return jnp.pad(total[:-1], ((1, 0), (0, 0), (0, 0)))


def shift_cells(source, row_shift, col_shift, grid_width):
    cell_count = source.shape[-1]
    margin = grid_width + 1
    padded = jnp.pad(source, [(0, 0)] * (source.ndim - 1) + [(margin, margin)])
    first_cell = margin + row_shift * grid_width + col_shift
    shifted = lax.slice_in_dim(padded, first_cell, first_cell + cell_count, axis=source.ndim - 1)
    column = jnp.arange(cell_count) % grid_width
    inside = (column + col_shift >= 0) & (column + col_shift < grid_width)
    return jnp.where(inside, shifted, jnp.zeros((), source.dtype))


def stencil_stack(source, grid_width, decay_factor):
    parts = [
        shift_cells(source, decay_factor * pair[0], decay_factor * pair[1], grid_width)
        for pair in offsets
    ]
    return jnp.stack(parts, axis=source.ndim - 2)


def stencil_conv(inputs, kernel, width):
    frames, chans, cells = inputs.shape
    image = inputs.reshape(frames, chans, cells // width, width)
    taps = kernel.reshape(3, 3, kernel.shape[1], chans).transpose(2, 3, 0, 1)
    out = lax.conv_general_dilated(
        image, taps, (1, 1), ((1, 1), (1, 1)), dimension_numbers=("NCHW", "OIHW", "NCHW"),
        preferred_element_type=jnp.float32,
    )
    return out.reshape(frames, kernel.shape[1], cells)


def gather_readout(cotangent, kernel_c, states_local, axis):
    count = lax.axis_size(axis)
    me = lax.axis_index(axis)
    cot_blocks = [cotangent]
    kernel_blocks = [lax.dynamic_slice_in_dim(kernel_c, me * states_local, states_local, axis=2)]
    for step in range(1, count):
        pairs = [(source, (source + step) % count) for source in range(count)]
        wanted = lax.dynamic_slice_in_dim(kernel_c, ((me + step) % count) * states_local, states_local, axis=2)
        cot_blocks.append(lax.ppermute(cotangent, axis, pairs))
        kernel_blocks.append(lax.ppermute(wanted, axis, pairs))
    return jnp.concatenate(cot_blocks, axis=1), jnp.concatenate(kernel_blocks, axis=1)


def gather_by_permutes(value, axis):
    count = lax.axis_size(axis)
    me = lax.axis_index(axis)
    by_step = [value]
    for step in range(1, count):
        by_step.append(lax.ppermute(value, axis, [(source, (source + step) % count) for source in range(count)]))
    by_source = jnp.take(jnp.stack(by_step), (me - jnp.arange(count)) % count, axis=0)
    return jnp.moveaxis(by_source, 0, 1).reshape(value.shape[0], count * value.shape[1], *value.shape[2:])


FRAME_AXES = ("chip", "core")


def pair_then_chip_sum(first, second):
    core = lax.axis_index("core")
    swap = [(0, 1), (1, 0)]
    first_flat, second_flat = first.reshape(-1), second.reshape(-1)
    kept = jnp.where(core == 0, first_flat, second_flat)
    sent = jnp.where(core == 0, second_flat, first_flat)
    pair_sum = (kept + lax.ppermute(sent, "core", swap)).reshape(lax.axis_size("chip"), -1)
    pieces = lax.all_to_all(pair_sum, "chip", 0, 0, tiled=True)
    reduced = jnp.sum(pieces, axis=0, keepdims=True)
    total = lax.all_to_all(jnp.broadcast_to(reduced, pieces.shape), "chip", 0, 0, tiled=True).reshape(-1)
    partner = lax.ppermute(total, "core", swap)
    first_total = jnp.where(core == 0, total, partner)
    second_total = jnp.where(core == 0, partner, total)
    return first_total.reshape(first.shape), second_total.reshape(second.shape)


def body(inputs, decay, kernel_b, kernel_c, cotangent):
    local_rows = kernel_b.shape[1]
    cell_count = inputs.shape[-1]
    blank_state = jnp.zeros((local_rows, cell_count), jnp.float32)
    drives = stencil_conv(inputs, kernel_b, W)

    def advance(current, frame_pair):
        frame_rate, drive = frame_pair
        current = frame_rate[:, None] * current + drive
        return (current, current)

    local_end, local_states = lax.scan(advance, blank_state, (decay, drives))
    decay_total = jnp.prod(decay, axis=0)
    blocks = lax.axis_size(FRAME_AXES)
    rows = local_end.shape[0]
    chunk = rows // blocks
    entering_owned = scan_owned(lax.all_to_all(pack_chunks(decay_total, local_end, blocks), FRAME_AXES, 0, 0, tiled=True), False)
    cot_stack = stencil_stack(cotangent, W, -1)
    all_cotangent, readout_local = gather_readout(cotangent, kernel_c, kernel_b.shape[1], "chan")
    injected = stencil_conv(all_cotangent, jnp.flip(readout_local, 0).transpose(0, 2, 1), W)
    entering_owned, injected = lax.optimization_barrier((entering_owned, injected))

    def retreat(carried, frame_pair):
        frame_rate, source = frame_pair
        adjoint = source + carried
        return (frame_rate[:, None] * adjoint, adjoint)

    message, local_adjoint = lax.scan(retreat, blank_state, (decay, injected), reverse=True)

    exchanged = lax.all_to_all(
        jnp.concatenate([entering_owned, pack_chunks(decay_total, message, blocks)], axis=1), FRAME_AXES, 0, 0, tiled=True
    )
    entering = exchanged[:, :chunk].reshape(rows, cell_count)
    arriving_owned = scan_owned(exchanged[:, chunk:], True)
    arriving = lax.all_to_all(arriving_owned, FRAME_AXES, 0, 0, tiled=True).reshape(rows, cell_count)
    cumulative = jnp.cumprod(decay, axis=0)
    states = local_states + cumulative[:, :, None] * entering[None]
    previous = jnp.concatenate([entering[None], states[:-1]], axis=0)
    states_bf = states.astype(jnp.bfloat16)
    suffix = jnp.flip(jnp.cumprod(jnp.flip(decay, 0), 0), 0)
    later_decay = jnp.concatenate([suffix[1:], jnp.ones_like(decay[:1])], axis=0)
    adjoint = local_adjoint + later_decay[:, :, None] * arriving[None]
    decay_grad = jnp.sum(adjoint * previous, axis=2)
    adjoint_bf = adjoint.astype(jnp.bfloat16)
    input_stack = stencil_stack(inputs, W, 1)
    grad_b_part = jnp.einsum(
        "fps,fkcs->kpc", adjoint_bf, input_stack, preferred_element_type=jnp.float32
    )
    all_states = gather_by_permutes(states_bf, "chan")
    grad_c_part = jnp.einsum(
        "fkus,fps->kup", cot_stack, all_states, preferred_element_type=jnp.float32
    )
    grad_b, grad_c = pair_then_chip_sum(grad_b_part, grad_c_part)
    return (grad_b, grad_c, decay_grad)


def solution(mesh):
    chan = mesh.shape["chan"]
    frame_mesh = Mesh(mesh.devices.reshape(-1, 2, chan), (*FRAME_AXES, "chan"))
    in_specs = (
        P(FRAME_AXES, None, None),
        P(FRAME_AXES, "chan"),
        P(None, "chan", None),
        P(None, "chan", None),
        P(FRAME_AXES, "chan", None),
    )
    out_specs = (P(None, "chan", None), P(None, "chan", None), P(FRAME_AXES, "chan"))
    return jax.shard_map(body, mesh=frame_mesh, in_specs=in_specs, out_specs=out_specs, check_vma=False)
```

```python
import jax
import jax.numpy as jnp
from jax import lax
from jax.sharding import Mesh, PartitionSpec as P

W = 64


offsets = ((-1, -1), (-1, 0), (-1, 1), (0, -1), (0, 0), (0, 1), (1, -1), (1, 0), (1, 1))


def passed_along(value, axis, steps):
    count = lax.axis_size(axis)
    first, last = (max(0, -steps), min(count, count - steps))
    return lax.ppermute(value, axis, [(source, source + steps) for source in range(first, last)])


def scan_chunks(factor, value, reverse):
    count = value.shape[0]
    distance = 1
    while distance < count:
        if reverse:
            pads = ((0, distance), (0, 0), (0, 0))
            earlier_value = jnp.pad(value[distance:], pads)
            earlier_factor = jnp.pad(factor[distance:], pads)
        else:
            pads = ((distance, 0), (0, 0), (0, 0))
            earlier_value = jnp.pad(value[:-distance], pads)
            earlier_factor = jnp.pad(factor[:-distance], pads)
        value = value + factor * earlier_value
        factor = factor * earlier_factor
        distance *= 2
    return value


def pack_chunks(factor, value, count):
    rows, cells = value.shape
    chunk = rows // count
    factor_row = jnp.pad(factor.reshape(count, chunk), ((0, 0), (0, cells - chunk)))[:, None, :]
    return jnp.concatenate([value.reshape(count, chunk, cells), factor_row], axis=1)


def scan_owned(gathered, reverse):
    chunk = gathered.shape[1] - 1
    total = scan_chunks(gathered[:, chunk, :chunk][:, :, None], gathered[:, :chunk], reverse)
    if reverse:
        return jnp.pad(total[1:], ((0, 1), (0, 0), (0, 0)))
    return jnp.pad(total[:-1], ((1, 0), (0, 0), (0, 0)))


def shift_cells(source, row_shift, col_shift, grid_width):
    cell_count = source.shape[-1]
    margin = grid_width + 1
    padded = jnp.pad(source, [(0, 0)] * (source.ndim - 1) + [(margin, margin)])
    first_cell = margin + row_shift * grid_width + col_shift
    shifted = lax.slice_in_dim(padded, first_cell, first_cell + cell_count, axis=source.ndim - 1)
    column = jnp.arange(cell_count) % grid_width
    inside = (column + col_shift >= 0) & (column + col_shift < grid_width)
    return jnp.where(inside, shifted, jnp.zeros((), source.dtype))


def stencil_stack(source, grid_width, decay_factor):
    parts = [
        shift_cells(source, decay_factor * pair[0], decay_factor * pair[1], grid_width)
        for pair in offsets
    ]
    return jnp.stack(parts, axis=source.ndim - 2)


def stencil_conv(inputs, kernel, width):
    frames, chans, cells = inputs.shape
    image = inputs.reshape(frames, chans, cells // width, width)
    taps = kernel.reshape(3, 3, kernel.shape[1], chans).transpose(2, 3, 0, 1)
    out = lax.conv_general_dilated(
        image, taps, (1, 1), ((1, 1), (1, 1)), dimension_numbers=("NCHW", "OIHW", "NCHW"),
        preferred_element_type=jnp.float32,
    )
    return out.reshape(frames, kernel.shape[1], cells)


def gather_readout(cotangent, kernel_c, states_local, axis):
    count = lax.axis_size(axis)
    me = lax.axis_index(axis)
    cot_blocks = [cotangent]
    kernel_blocks = [lax.dynamic_slice_in_dim(kernel_c, me * states_local, states_local, axis=2)]
    for step in range(1, count):
        pairs = [(source, (source + step) % count) for source in range(count)]
        wanted = lax.dynamic_slice_in_dim(kernel_c, ((me + step) % count) * states_local, states_local, axis=2)
        cot_blocks.append(lax.ppermute(cotangent, axis, pairs))
        kernel_blocks.append(lax.ppermute(wanted, axis, pairs))
    return jnp.concatenate(cot_blocks, axis=1), jnp.concatenate(kernel_blocks, axis=1)


def gather_by_permutes(value, axis):
    count = lax.axis_size(axis)
    me = lax.axis_index(axis)
    by_step = [value]
    for step in range(1, count):
        by_step.append(lax.ppermute(value, axis, [(source, (source + step) % count) for source in range(count)]))
    by_source = jnp.take(jnp.stack(by_step), (me - jnp.arange(count)) % count, axis=0)
    return jnp.moveaxis(by_source, 0, 1).reshape(value.shape[0], count * value.shape[1], *value.shape[2:])


FRAME_AXES = ("chip", "core")


def pair_then_chip_sum(first, second):
    core = lax.axis_index("core")
    chips = lax.axis_size("chip")
    swap = [(0, 1), (1, 0)]
    shape = (chips, first.size // (chips * first.shape[-1]), first.shape[-1])
    first_rows, second_rows = first.reshape(shape), second.reshape(shape)
    kept = jnp.where(core == 0, first_rows, second_rows)
    sent = jnp.where(core == 0, second_rows, first_rows)
    pair_sum = kept + lax.ppermute(sent, "core", swap)
    pieces = lax.all_to_all(pair_sum, "chip", 0, 0, tiled=True)
    reduced = jnp.sum(pieces, axis=0, keepdims=True)
    total = lax.all_to_all(jnp.broadcast_to(reduced, pieces.shape), "chip", 0, 0, tiled=True)
    partner = lax.ppermute(total, "core", swap)
    first_total = jnp.where(core == 0, total, partner)
    second_total = jnp.where(core == 0, partner, total)
    return first_total.reshape(first.shape), second_total.reshape(second.shape)


def body(inputs, decay, kernel_b, kernel_c, cotangent):
    local_rows = kernel_b.shape[1]
    cell_count = inputs.shape[-1]
    blank_state = jnp.zeros((local_rows, cell_count), jnp.float32)
    drives = stencil_conv(inputs, kernel_b, W)

    def advance(current, frame_pair):
        frame_rate, drive = frame_pair
        current = frame_rate[:, None] * current + drive
        return (current, current)

    local_end, local_states = lax.scan(advance, blank_state, (decay, drives))
    decay_total = jnp.prod(decay, axis=0)
    blocks = lax.axis_size(FRAME_AXES)
    rows = local_end.shape[0]
    chunk = rows // blocks
    entering_owned = scan_owned(lax.all_to_all(pack_chunks(decay_total, local_end, blocks), FRAME_AXES, 0, 0, tiled=True), False)
    cot_stack = stencil_stack(cotangent, W, -1)
    all_cotangent, readout_local = gather_readout(cotangent, kernel_c, kernel_b.shape[1], "chan")
    injected = stencil_conv(all_cotangent, jnp.flip(readout_local, 0).transpose(0, 2, 1), W)
    entering_owned, injected = lax.optimization_barrier((entering_owned, injected))

    def retreat(carried, frame_pair):
        frame_rate, source = frame_pair
        adjoint = source + carried
        return (frame_rate[:, None] * adjoint, adjoint)

    message, local_adjoint = lax.scan(retreat, blank_state, (decay, injected), reverse=True)

    exchanged = lax.all_to_all(
        jnp.concatenate([entering_owned, pack_chunks(decay_total, message, blocks)], axis=1), FRAME_AXES, 0, 0, tiled=True
    )
    entering = exchanged[:, :chunk].reshape(rows, cell_count)
    arriving_owned = scan_owned(exchanged[:, chunk:], True)
    arriving = lax.all_to_all(arriving_owned, FRAME_AXES, 0, 0, tiled=True).reshape(rows, cell_count)
    cumulative = jnp.cumprod(decay, axis=0)
    states = local_states + cumulative[:, :, None] * entering[None]
    previous = jnp.concatenate([entering[None], states[:-1]], axis=0)
    states_bf = states.astype(jnp.bfloat16)
    suffix = jnp.flip(jnp.cumprod(jnp.flip(decay, 0), 0), 0)
    later_decay = jnp.concatenate([suffix[1:], jnp.ones_like(decay[:1])], axis=0)
    adjoint = local_adjoint + later_decay[:, :, None] * arriving[None]
    decay_grad = jnp.sum(adjoint * previous, axis=2)
    adjoint_bf = adjoint.astype(jnp.bfloat16)
    input_stack = stencil_stack(inputs, W, 1)
    grad_b_part = jnp.einsum(
        "fps,fkcs->kpc", adjoint_bf, input_stack, preferred_element_type=jnp.float32
    )
    all_states = gather_by_permutes(states_bf, "chan")
    grad_c_part = jnp.einsum(
        "fkus,fps->kup", cot_stack, all_states, preferred_element_type=jnp.float32
    )
    grad_b, grad_c = pair_then_chip_sum(grad_b_part, grad_c_part)
    return (grad_b, grad_c, decay_grad)


def solution(mesh):
    chan = mesh.shape["chan"]
    frame_mesh = Mesh(mesh.devices.reshape(-1, 2, chan), (*FRAME_AXES, "chan"))
    in_specs = (
        P(FRAME_AXES, None, None),
        P(FRAME_AXES, "chan"),
        P(None, "chan", None),
        P(None, "chan", None),
        P(FRAME_AXES, "chan", None),
    )
    out_specs = (P(None, "chan", None), P(None, "chan", None), P(FRAME_AXES, "chan"))
    return jax.shard_map(body, mesh=frame_mesh, in_specs=in_specs, out_specs=out_specs, check_vma=False)
```

```python
import jax
import jax.numpy as jnp
from jax import lax
from jax.sharding import Mesh, PartitionSpec as P

W = 64


offsets = ((-1, -1), (-1, 0), (-1, 1), (0, -1), (0, 0), (0, 1), (1, -1), (1, 0), (1, 1))


def passed_along(value, axis, steps):
    count = lax.axis_size(axis)
    first, last = (max(0, -steps), min(count, count - steps))
    return lax.ppermute(value, axis, [(source, source + steps) for source in range(first, last)])


def scan_chunks(factor, value, reverse):
    count = value.shape[0]
    distance = 1
    while distance < count:
        if reverse:
            pads = ((0, distance), (0, 0), (0, 0))
            earlier_value = jnp.pad(value[distance:], pads)
            earlier_factor = jnp.pad(factor[distance:], pads)
        else:
            pads = ((distance, 0), (0, 0), (0, 0))
            earlier_value = jnp.pad(value[:-distance], pads)
            earlier_factor = jnp.pad(factor[:-distance], pads)
        value = value + factor * earlier_value
        factor = factor * earlier_factor
        distance *= 2
    return value


def pack_chunks(factor, value, count):
    rows, cells = value.shape
    chunk = rows // count
    factor_row = jnp.pad(factor.reshape(count, chunk), ((0, 0), (0, cells - chunk)))[:, None, :]
    return jnp.concatenate([value.reshape(count, chunk, cells), factor_row], axis=1)


def scan_owned(gathered, reverse):
    chunk = gathered.shape[1] - 1
    total = scan_chunks(gathered[:, chunk, :chunk][:, :, None], gathered[:, :chunk], reverse)
    if reverse:
        return jnp.pad(total[1:], ((0, 1), (0, 0), (0, 0)))
    return jnp.pad(total[:-1], ((1, 0), (0, 0), (0, 0)))


def shift_cells(source, row_shift, col_shift, grid_width):
    cell_count = source.shape[-1]
    margin = grid_width + 1
    padded = jnp.pad(source, [(0, 0)] * (source.ndim - 1) + [(margin, margin)])
    first_cell = margin + row_shift * grid_width + col_shift
    shifted = lax.slice_in_dim(padded, first_cell, first_cell + cell_count, axis=source.ndim - 1)
    column = jnp.arange(cell_count) % grid_width
    inside = (column + col_shift >= 0) & (column + col_shift < grid_width)
    return jnp.where(inside, shifted, jnp.zeros((), source.dtype))


def stencil_stack(source, grid_width, decay_factor):
    parts = [
        shift_cells(source, decay_factor * pair[0], decay_factor * pair[1], grid_width)
        for pair in offsets
    ]
    return jnp.stack(parts, axis=source.ndim - 2)


def stencil_conv(inputs, kernel, width):
    frames, chans, cells = inputs.shape
    image = inputs.reshape(frames, chans, cells // width, width)
    taps = kernel.reshape(3, 3, kernel.shape[1], chans).transpose(2, 3, 0, 1)
    out = lax.conv_general_dilated(
        image, taps, (1, 1), ((1, 1), (1, 1)), dimension_numbers=("NCHW", "OIHW", "NCHW"),
        preferred_element_type=jnp.float32,
    )
    return out.reshape(frames, kernel.shape[1], cells)


def gather_readout(cotangent, kernel_c, states_local, axis):
    count = lax.axis_size(axis)
    me = lax.axis_index(axis)
    cot_blocks = [cotangent]
    kernel_blocks = [lax.dynamic_slice_in_dim(kernel_c, me * states_local, states_local, axis=2)]
    for step in range(1, count):
        pairs = [(source, (source + step) % count) for source in range(count)]
        wanted = lax.dynamic_slice_in_dim(kernel_c, ((me + step) % count) * states_local, states_local, axis=2)
        cot_blocks.append(lax.ppermute(cotangent, axis, pairs))
        kernel_blocks.append(lax.ppermute(wanted, axis, pairs))
    return jnp.concatenate(cot_blocks, axis=1), jnp.concatenate(kernel_blocks, axis=1)


def gather_by_permutes(value, axis):
    count = lax.axis_size(axis)
    me = lax.axis_index(axis)
    by_step = [value]
    for step in range(1, count):
        by_step.append(lax.ppermute(value, axis, [(source, (source + step) % count) for source in range(count)]))
    by_source = jnp.take(jnp.stack(by_step), (me - jnp.arange(count)) % count, axis=0)
    return jnp.moveaxis(by_source, 0, 1).reshape(value.shape[0], count * value.shape[1], *value.shape[2:])


FRAME_AXES = ("chip", "core")


def pair_then_chip_sum(first, second):
    core = lax.axis_index("core")
    chips = lax.axis_size("chip")
    swap = [(0, 1), (1, 0)]
    shape = (chips, first.size // (chips * first.shape[-1]), first.shape[-1])
    first_rows, second_rows = first.reshape(shape), second.reshape(shape)
    kept = jnp.where(core == 0, first_rows, second_rows)
    sent = jnp.where(core == 0, second_rows, first_rows)
    pair_sum = kept + lax.ppermute(sent, "core", swap)
    pieces = lax.all_to_all(pair_sum, "chip", 0, 0, tiled=True)
    reduced = jnp.sum(pieces, axis=0, keepdims=True)
    total = lax.all_to_all(jnp.broadcast_to(reduced, pieces.shape), "chip", 0, 0, tiled=True)
    partner = lax.ppermute(total, "core", swap)
    first_total = jnp.where(core == 0, total, partner)
    second_total = jnp.where(core == 0, partner, total)
    return first_total.reshape(first.shape), second_total.reshape(second.shape)


def body(inputs, decay, kernel_b, kernel_c, cotangent):
    local_rows = kernel_b.shape[1]
    cell_count = inputs.shape[-1]
    blank_state = jnp.zeros((local_rows, cell_count), jnp.float32)
    drives = stencil_conv(inputs, kernel_b, W)

    def advance(current, frame_pair):
        frame_rate, drive = frame_pair
        current = frame_rate[:, None] * current + drive
        return (current, current)

    local_end, local_states = lax.scan(advance, blank_state, (decay, drives), unroll=True)
    decay_total = jnp.prod(decay, axis=0)
    blocks = lax.axis_size(FRAME_AXES)
    rows = local_end.shape[0]
    chunk = rows // blocks
    entering_owned = scan_owned(lax.all_to_all(pack_chunks(decay_total, local_end, blocks), FRAME_AXES, 0, 0, tiled=True), False)
    cot_stack = stencil_stack(cotangent, W, -1)
    all_cotangent, readout_local = gather_readout(cotangent, kernel_c, kernel_b.shape[1], "chan")
    injected = stencil_conv(all_cotangent, jnp.flip(readout_local, 0).transpose(0, 2, 1), W)
    entering_owned, injected = lax.optimization_barrier((entering_owned, injected))

    def retreat(carried, frame_pair):
        frame_rate, source = frame_pair
        adjoint = source + carried
        return (frame_rate[:, None] * adjoint, adjoint)

    message, local_adjoint = lax.scan(retreat, blank_state, (decay, injected), reverse=True, unroll=True)

    exchanged = lax.all_to_all(
        jnp.concatenate([entering_owned, pack_chunks(decay_total, message, blocks)], axis=1), FRAME_AXES, 0, 0, tiled=True
    )
    entering = exchanged[:, :chunk].reshape(rows, cell_count)
    arriving_owned = scan_owned(exchanged[:, chunk:], True)
    arriving = lax.all_to_all(arriving_owned, FRAME_AXES, 0, 0, tiled=True).reshape(rows, cell_count)
    cumulative = jnp.cumprod(decay, axis=0)
    states = local_states + cumulative[:, :, None] * entering[None]
    previous = jnp.concatenate([entering[None], states[:-1]], axis=0)
    states_bf = states.astype(jnp.bfloat16)
    suffix = jnp.flip(jnp.cumprod(jnp.flip(decay, 0), 0), 0)
    later_decay = jnp.concatenate([suffix[1:], jnp.ones_like(decay[:1])], axis=0)
    adjoint = local_adjoint + later_decay[:, :, None] * arriving[None]
    decay_grad = jnp.sum(adjoint * previous, axis=2)
    adjoint_bf = adjoint.astype(jnp.bfloat16)
    input_stack = stencil_stack(inputs, W, 1)
    grad_b_part = jnp.einsum(
        "fps,fkcs->kpc", adjoint_bf, input_stack, preferred_element_type=jnp.float32
    )
    all_states = gather_by_permutes(states_bf, "chan")
    grad_c_part = jnp.einsum(
        "fkus,fps->kup", cot_stack, all_states, preferred_element_type=jnp.float32
    )
    grad_b, grad_c = pair_then_chip_sum(grad_b_part, grad_c_part)
    return (grad_b, grad_c, decay_grad)


def solution(mesh):
    chan = mesh.shape["chan"]
    frame_mesh = Mesh(mesh.devices.reshape(-1, 2, chan), (*FRAME_AXES, "chan"))
    in_specs = (
        P(FRAME_AXES, None, None),
        P(FRAME_AXES, "chan"),
        P(None, "chan", None),
        P(None, "chan", None),
        P(FRAME_AXES, "chan", None),
    )
    out_specs = (P(None, "chan", None), P(None, "chan", None), P(FRAME_AXES, "chan"))
    return jax.shard_map(body, mesh=frame_mesh, in_specs=in_specs, out_specs=out_specs, check_vma=False)
```

```python
import jax
import jax.numpy as jnp
from jax import lax
from jax.sharding import Mesh, PartitionSpec as P

W = 64


offsets = ((-1, -1), (-1, 0), (-1, 1), (0, -1), (0, 0), (0, 1), (1, -1), (1, 0), (1, 1))


def passed_along(value, axis, steps):
    count = lax.axis_size(axis)
    first, last = (max(0, -steps), min(count, count - steps))
    return lax.ppermute(value, axis, [(source, source + steps) for source in range(first, last)])


def scan_chunks(factor, value, reverse):
    count = value.shape[0]
    distance = 1
    while distance < count:
        if reverse:
            pads = ((0, distance), (0, 0), (0, 0))
            earlier_value = jnp.pad(value[distance:], pads)
            earlier_factor = jnp.pad(factor[distance:], pads)
        else:
            pads = ((distance, 0), (0, 0), (0, 0))
            earlier_value = jnp.pad(value[:-distance], pads)
            earlier_factor = jnp.pad(factor[:-distance], pads)
        value = value + factor * earlier_value
        factor = factor * earlier_factor
        distance *= 2
    return value


def pack_chunks(factor, value, count):
    rows, cells = value.shape
    chunk = rows // count
    factor_row = jnp.pad(factor.reshape(count, chunk), ((0, 0), (0, cells - chunk)))[:, None, :]
    return jnp.concatenate([value.reshape(count, chunk, cells), factor_row], axis=1)


def scan_owned(gathered, reverse):
    chunk = gathered.shape[1] - 1
    total = scan_chunks(gathered[:, chunk, :chunk][:, :, None], gathered[:, :chunk], reverse)
    if reverse:
        return jnp.pad(total[1:], ((0, 1), (0, 0), (0, 0)))
    return jnp.pad(total[:-1], ((1, 0), (0, 0), (0, 0)))


def shift_cells(source, row_shift, col_shift, grid_width):
    cell_count = source.shape[-1]
    margin = grid_width + 1
    padded = jnp.pad(source, [(0, 0)] * (source.ndim - 1) + [(margin, margin)])
    first_cell = margin + row_shift * grid_width + col_shift
    shifted = lax.slice_in_dim(padded, first_cell, first_cell + cell_count, axis=source.ndim - 1)
    column = jnp.arange(cell_count) % grid_width
    inside = (column + col_shift >= 0) & (column + col_shift < grid_width)
    return jnp.where(inside, shifted, jnp.zeros((), source.dtype))


def stencil_stack(source, grid_width, decay_factor):
    parts = [
        shift_cells(source, decay_factor * pair[0], decay_factor * pair[1], grid_width)
        for pair in offsets
    ]
    return jnp.stack(parts, axis=source.ndim - 2)


def stencil_conv(inputs, kernel, width):
    frames, chans, cells = inputs.shape
    image = inputs.reshape(frames, chans, cells // width, width)
    taps = kernel.reshape(3, 3, kernel.shape[1], chans).transpose(2, 3, 0, 1)
    out = lax.conv_general_dilated(
        image, taps, (1, 1), ((1, 1), (1, 1)), dimension_numbers=("NCHW", "OIHW", "NCHW"),
        preferred_element_type=jnp.float32,
    )
    return out.reshape(frames, kernel.shape[1], cells)


def gather_readout(cotangent, kernel_c, states_local, axis):
    count = lax.axis_size(axis)
    me = lax.axis_index(axis)
    cot_blocks = [cotangent]
    kernel_blocks = [lax.dynamic_slice_in_dim(kernel_c, me * states_local, states_local, axis=2)]
    for step in range(1, count):
        pairs = [(source, (source + step) % count) for source in range(count)]
        wanted = lax.dynamic_slice_in_dim(kernel_c, ((me + step) % count) * states_local, states_local, axis=2)
        cot_blocks.append(lax.ppermute(cotangent, axis, pairs))
        kernel_blocks.append(lax.ppermute(wanted, axis, pairs))
    return jnp.concatenate(cot_blocks, axis=1), jnp.concatenate(kernel_blocks, axis=1)


def gather_by_permutes(value, axis):
    count = lax.axis_size(axis)
    me = lax.axis_index(axis)
    by_step = [value]
    for step in range(1, count):
        by_step.append(lax.ppermute(value, axis, [(source, (source + step) % count) for source in range(count)]))
    by_source = jnp.take(jnp.stack(by_step), (me - jnp.arange(count)) % count, axis=0)
    return jnp.moveaxis(by_source, 0, 1).reshape(value.shape[0], count * value.shape[1], *value.shape[2:])


FRAME_AXES = ("chip", "core")


def pair_then_chip_sum(first, second):
    core = lax.axis_index("core")
    chips = lax.axis_size("chip")
    swap = [(0, 1), (1, 0)]
    shape = (chips, first.size // (chips * first.shape[-1]), first.shape[-1])
    first_rows, second_rows = first.reshape(shape), second.reshape(shape)
    kept = jnp.where(core == 0, first_rows, second_rows)
    sent = jnp.where(core == 0, second_rows, first_rows)
    pair_sum = kept + lax.ppermute(sent, "core", swap)
    pieces = lax.all_to_all(pair_sum, "chip", 0, 0, tiled=True)
    reduced = jnp.sum(pieces, axis=0, keepdims=True)
    total = lax.all_to_all(jnp.broadcast_to(reduced, pieces.shape), "chip", 0, 0, tiled=True)
    partner = lax.ppermute(total, "core", swap)
    first_total = jnp.where(core == 0, total, partner)
    second_total = jnp.where(core == 0, partner, total)
    return first_total.reshape(first.shape), second_total.reshape(second.shape)


def body(inputs, decay, kernel_b, kernel_c, cotangent):
    local_rows = kernel_b.shape[1]
    cell_count = inputs.shape[-1]
    blank_state = jnp.zeros((local_rows, cell_count), jnp.float32)
    drives = stencil_conv(inputs, kernel_b, W)

    def advance(current, frame_pair):
        frame_rate, drive = frame_pair
        current = frame_rate[:, None] * current + drive
        return (current, current)

    local_end, local_states = lax.scan(advance, blank_state, (decay, drives))
    decay_total = jnp.prod(decay, axis=0)
    blocks = lax.axis_size(FRAME_AXES)
    rows = local_end.shape[0]
    chunk = rows // blocks
    entering_owned = scan_owned(lax.all_to_all(pack_chunks(decay_total, local_end, blocks), FRAME_AXES, 0, 0, tiled=True), False)
    cot_stack = stencil_stack(cotangent, W, -1)
    all_cotangent, readout_local = gather_readout(cotangent, kernel_c, kernel_b.shape[1], "chan")
    injected = stencil_conv(all_cotangent, jnp.flip(readout_local, 0).transpose(0, 2, 1), W)

    def retreat(carried, frame_pair):
        frame_rate, source = frame_pair
        adjoint = source + carried
        return (frame_rate[:, None] * adjoint, adjoint)

    message, local_adjoint = lax.scan(retreat, blank_state, (decay, injected), reverse=True)

    exchanged = lax.all_to_all(
        jnp.concatenate([entering_owned, pack_chunks(decay_total, message, blocks)], axis=1), FRAME_AXES, 0, 0, tiled=True
    )
    entering = exchanged[:, :chunk].reshape(rows, cell_count)
    arriving_owned = scan_owned(exchanged[:, chunk:], True)
    arriving = lax.all_to_all(arriving_owned, FRAME_AXES, 0, 0, tiled=True).reshape(rows, cell_count)
    cumulative = jnp.cumprod(decay, axis=0)
    states = local_states + cumulative[:, :, None] * entering[None]
    previous = jnp.concatenate([entering[None], states[:-1]], axis=0)
    states_bf = states.astype(jnp.bfloat16)
    suffix = jnp.flip(jnp.cumprod(jnp.flip(decay, 0), 0), 0)
    later_decay = jnp.concatenate([suffix[1:], jnp.ones_like(decay[:1])], axis=0)
    adjoint = local_adjoint + later_decay[:, :, None] * arriving[None]
    decay_grad = jnp.sum(adjoint * previous, axis=2)
    adjoint_bf = adjoint.astype(jnp.bfloat16)
    input_stack = stencil_stack(inputs, W, 1)
    grad_b_part = jnp.einsum(
        "fps,fkcs->kpc", adjoint_bf, input_stack, preferred_element_type=jnp.float32
    )
    all_states = gather_by_permutes(states_bf, "chan")
    grad_c_part = jnp.einsum(
        "fkus,fps->kup", cot_stack, all_states, preferred_element_type=jnp.float32
    )
    grad_b, grad_c = pair_then_chip_sum(grad_b_part, grad_c_part)
    return (grad_b, grad_c, decay_grad)


def solution(mesh):
    chan = mesh.shape["chan"]
    frame_mesh = Mesh(mesh.devices.reshape(-1, 2, chan), (*FRAME_AXES, "chan"))
    in_specs = (
        P(FRAME_AXES, None, None),
        P(FRAME_AXES, "chan"),
        P(None, "chan", None),
        P(None, "chan", None),
        P(FRAME_AXES, "chan", None),
    )
    out_specs = (P(None, "chan", None), P(None, "chan", None), P(FRAME_AXES, "chan"))
    return jax.shard_map(body, mesh=frame_mesh, in_specs=in_specs, out_specs=out_specs, check_vma=False)
```
